256 devices in a mesh: dp: 32 (over z, y), tensor: 8 (over x, core).
Axes of the slice: x: 4, y: 4, z: 8, core: 2. Of those that a mesh axis runs over, the one named last changes fastest.
Arguments:
- tokens: bfloat16 [4096, 4096], P('dp', 'tensor'), may hold values from -6 to 6
- grad_out: bfloat16 [4096, 4096], P('dp', 'tensor'), may hold values from -6 to 6
- gate_blocks: int32 [8, 32], P('tensor'), may hold values from -1 to 447, as said below
- gate_values: bfloat16 [8, 32, 128, 128], P('tensor'), may hold values from -0.375 to 0.375
- up_blocks: int32 [8, 32], P('tensor'), may hold values from -1 to 447, as said below
- up_values: bfloat16 [8, 32, 128, 128], P('tensor'), may hold values from -0.375 to 0.375
- down_blocks: int32 [8, 32], P('tensor'), may hold values from -1 to 447, as said below
- down_values: bfloat16 [8, 32, 128, 128], P('tensor'), may hold values from -0.1875 to 0.1875
Outputs:
- mixed: bfloat16 [4096, 4096], P('dp', 'tensor')
- grad_tokens: bfloat16 [4096, 4096], P('dp', 'tensor')
- grad_gate: float32 [8, 32, 128, 128], P('tensor', 'dp')
- grad_up: float32 [8, 32, 128, 128], P('tensor', 'dp')
- grad_down: float32 [8, 32, 128, 128], P('tensor', 'dp')
The draws below stay inside these ranges and needn't reach their ends.
Inputs may be any that keep to these rules, and one draw needn't show every extreme that they name: `gate_blocks`: each row lists distinct block numbers of one tensor shard in its first slots and -1 in the rest; a row has 16 to 32 listed blocks, one row has exactly 32 and another exactly 16. `up_blocks`: as for gate_blocks, drawn apart. `down_blocks`: as for gate_blocks, drawn apart.
All inputs are finite; a program needn't handle non-finite values.
Results may differ from the reference program's by a relative error of at most 0.015.
Values may be sent and summed in bfloat16 or wider, within the bound.
No kernel may reach another device: no remote copies, remote signals or barrier semaphores. Data moves between devices by JAX's collectives and lax.ppermute only.
A program may use at most 64 MiB of HBM per device.

```python
import jax
import jax.numpy as jnp
from jax import lax

BS = 128
D = 4096
SLOTS = 32
SHARDS = 8
RB = 32
CB = 14
BLOCKS = 448
TOKENS = 4096


def block_lists(key):
    perm_key, count_key, full_key, half_key = jax.random.split(key, 4)
    row_keys = jax.random.split(perm_key, SHARDS)
    perms = jax.vmap(lambda row_key: jax.random.permutation(row_key, BLOCKS))(row_keys).astype(jnp.int32)
    full_row = jax.random.randint(full_key, (), 0, SHARDS)
    half_row = (full_row + 1 + jax.random.randint(half_key, (), 0, SHARDS - 1)) % SHARDS
    shard_ids = jnp.arange(SHARDS)
    rotated = (perms + (BLOCKS - 1 - perms[:, :1])) % BLOCKS
    perms = jnp.where((shard_ids == full_row)[:, None], rotated, perms)[:, :SLOTS]
    counts = jax.random.randint(count_key, (SHARDS,), SLOTS // 2, SLOTS + 1)
    counts = jnp.where(shard_ids == full_row, SLOTS, jnp.where(shard_ids == half_row, SLOTS // 2, counts))
    position = jnp.arange(SLOTS)[None, :]
    return jnp.where(position < counts[:, None], perms, -1).astype(jnp.int32)


def draw_gate_blocks(key, part):
    return block_lists(jax.random.fold_in(key, 11))


def draw_up_blocks(key, part):
    return block_lists(jax.random.fold_in(key, 12))


def draw_down_blocks(key, part):
    return block_lists(jax.random.fold_in(key, 13))


def block_scale(rng, dims, cuts, least, largest):
    gain, own = 1.0, jax.random.fold_in(rng, 6)
    for dim, shards_of in cuts:
        heights = jnp.exp(jax.random.uniform(jax.random.fold_in(own, dim), (shards_of,), jnp.float32, least / len(cuts), largest / len(cuts)))
        gain = gain * jnp.repeat(heights, dims[dim] // shards_of).reshape([-1 if axis == dim else 1 for axis in range(len(dims))])
    return gain


def normal_values(own_key, extent, spread, bound, cuts=(), kind=jnp.bfloat16):
    drawn = jax.random.normal(own_key, extent, jnp.float32) * spread
    if len(cuts) > 0:
        drawn = block_scale(own_key, extent, cuts, -0.22, 0.18) * drawn
    return jnp.clip(drawn, min=-bound, max=bound).astype(kind)


def setup_inputs(seed: int = 0) -> dict:
    key_list = jax.random.split(jax.random.key(seed), 9)
    tokens = normal_values(key_list[0], (TOKENS, D), 1.0, 6.0, ((0, 32), (1, 8)))
    grad_out = normal_values(key_list[1], (TOKENS, D), 1.0, 6.0, ((0, 32), (1, 8)))
    gate_blocks = draw_gate_blocks(jax.random.fold_in(key_list[8], 71), 0)
    gate_values = normal_values(key_list[3], (SHARDS, SLOTS, BS, BS), (SLOTS * BS // CB) ** -0.5, 0.375, ((0, 8),))
    up_blocks = draw_up_blocks(jax.random.fold_in(key_list[8], 71), 0)
    up_values = normal_values(key_list[5], (SHARDS, SLOTS, BS, BS), (SLOTS * BS // CB) ** -0.5, 0.375, ((0, 8),))
    down_blocks = draw_down_blocks(jax.random.fold_in(key_list[8], 71), 0)
    down_values = normal_values(key_list[7], (SHARDS, SLOTS, BS, BS), (SLOTS * BS * SHARDS // RB) ** -0.5, 0.1875, ((0, 8),))
    return {"tokens": tokens, "grad_out": grad_out, "gate_blocks": gate_blocks, "gate_values": gate_values, "up_blocks": up_blocks, "up_values": up_values, "down_blocks": down_blocks, "down_values": down_values}


def locate(blocks):
    safe = jnp.maximum(blocks, 0)
    hidden_at = (safe // RB).astype(jnp.int32)
    feature_at = (safe % RB).astype(jnp.int32)
    weight = (blocks >= 0).astype(jnp.float32)
    return hidden_at, feature_at, weight


def accumulate(source, values, take_at, put_at, weight, count, flip):
    start_total = jnp.zeros((source.shape[0], count, source.shape[2]), jnp.float32)

    def advance(total, item):
        block_values, source_at, target_at, scale = item
        piece = lax.dynamic_index_in_dim(source, source_at, 1, keepdims=False)
        matrix = block_values.T if flip else block_values
        term = jnp.dot(piece, matrix, preferred_element_type=jnp.float32) * scale
        current = lax.dynamic_index_in_dim(total, target_at, 1, keepdims=False)
        return lax.dynamic_update_index_in_dim(total, current + term, target_at, 1), None

    return lax.scan(advance, start_total, (values, take_at, put_at, weight))[0]


def block_grads(left, right, left_at, right_at, weight):
    def single(item):
        first_at, second_at, scale = item
        first = lax.dynamic_index_in_dim(left, first_at, 1, keepdims=False)
        second = lax.dynamic_index_in_dim(right, second_at, 1, keepdims=False)
        return jnp.dot(first.T, second, preferred_element_type=jnp.float32) * scale

    return lax.map(single, (left_at, right_at, weight))


def reference(tokens, grad_out, gate_blocks, gate_values, up_blocks, up_values, down_blocks, down_values):
    inputs = tokens.reshape(TOKENS, RB, BS)
    upstream = grad_out.reshape(TOKENS, RB, BS)
    mixed_total = jnp.zeros((TOKENS, D), jnp.float32)
    input_total = jnp.zeros((TOKENS, D), jnp.float32)
    gate_list, up_list, down_list = [], [], []
    for shard in range(SHARDS):
        gate_hid, gate_feat, gate_live = locate(gate_blocks[shard])
        up_hid, up_feat, up_live = locate(up_blocks[shard])
        down_hid, down_feat, down_live = locate(down_blocks[shard])
        gate_pre = accumulate(inputs, gate_values[shard], gate_feat, gate_hid, gate_live, CB, False)
        up_pre = accumulate(inputs, up_values[shard], up_feat, up_hid, up_live, CB, False)
        sigma_gate = jax.nn.sigmoid(gate_pre)
        activated = gate_pre * sigma_gate
        hidden = (activated * up_pre).astype(jnp.bfloat16)
        mixed_part = accumulate(hidden, down_values[shard], down_hid, down_feat, down_live, RB, False)
        rounded = lax.optimization_barrier(mixed_part.reshape(TOKENS, D).astype(jnp.bfloat16))
        mixed_total = mixed_total + rounded.astype(jnp.float32)
        hidden_grad = accumulate(upstream, down_values[shard], down_feat, down_hid, down_live, CB, True)
        gate_delta = (hidden_grad * up_pre * sigma_gate * (1.0 + gate_pre * (1.0 - sigma_gate))).astype(jnp.bfloat16)
        up_delta = (hidden_grad * activated).astype(jnp.bfloat16)
        input_part = accumulate(gate_delta, gate_values[shard], gate_hid, gate_feat, gate_live, RB, True)
        input_part = input_part + accumulate(up_delta, up_values[shard], up_hid, up_feat, up_live, RB, True)
        rounded_input = lax.optimization_barrier(input_part.reshape(TOKENS, D).astype(jnp.bfloat16))
        input_total = input_total + rounded_input.astype(jnp.float32)
        gate_list.append(block_grads(inputs, gate_delta, gate_feat, gate_hid, gate_live))
        up_list.append(block_grads(inputs, up_delta, up_feat, up_hid, up_live))
        down_list.append(block_grads(hidden, upstream, down_hid, down_feat, down_live))
    return (mixed_total.astype(jnp.bfloat16), input_total.astype(jnp.bfloat16),
            jnp.stack(gate_list), jnp.stack(up_list), jnp.stack(down_list))
```

```python
import jax
import jax.numpy as jnp
from jax import lax
from jax.sharding import PartitionSpec as P

FF = 14336


def locate(blocks, feature_count):
    flat = blocks[0]
    weight = (flat >= 0).astype(jnp.float32)
    safe = jnp.maximum(flat, 0)
    return (safe // feature_count, safe % feature_count, weight)


def one_hot(targets, weight, count):
    return (targets[:, None] == jnp.arange(count)[None, :]).astype(jnp.float32) * weight[:, None]


def spread(product, table):
    return jnp.einsum("tsn,sc->tcn", product, table, precision=lax.Precision.HIGHEST)


def select(source, position):
    return jnp.take(source, position, axis=1)


def forward_blocks(rows_in, values):
    return jnp.einsum("tsk,skn->tsn", rows_in, values, preferred_element_type=jnp.float32)


def backward_blocks(rows_in, values):
    return jnp.einsum("tsn,skn->tsk", rows_in, values, preferred_element_type=jnp.float32)


def slot_term(left, right, weight):
    product = jnp.einsum("tsk,tsn->skn", left, right, preferred_element_type=jnp.float32)
    return product * weight[:, None, None]


def body(
    tokens, grad_out, gate_blocks, gate_values, up_blocks, up_values, down_blocks, down_values
):
    gathered_x, gathered_dy = (
        lax.all_gather(tokens, "tensor", axis=1, tiled=True),
        lax.all_gather(grad_out, "tensor", axis=1, tiled=True),
    )
    tok_rows, feature_width = gathered_x.shape
    block_size = gate_values.shape[-1]
    feature_count = feature_width // block_size
    hidden_count = FF // (block_size * lax.axis_size("tensor"))
    inputs = gathered_x.reshape(tok_rows, feature_count, block_size)
    upstream = gathered_dy.reshape(tok_rows, feature_count, block_size)
    gate_hid, gate_feat, gate_live = locate(gate_blocks, feature_count)
    up_hid, up_feat, up_live = locate(up_blocks, feature_count)
    down_hid, down_feat, down_live = locate(down_blocks, feature_count)
    gate_rows = select(inputs, gate_feat)
    up_rows = select(inputs, up_feat)
    gate_pre = spread(
        forward_blocks(gate_rows, gate_values[0]), one_hot(gate_hid, gate_live, hidden_count)
    )
    up_pre = spread(forward_blocks(up_rows, up_values[0]), one_hot(up_hid, up_live, hidden_count))
    sigma_gate = jax.nn.sigmoid(gate_pre)
    activated = gate_pre * sigma_gate
    hidden = (activated * up_pre).astype(jnp.bfloat16)
    hidden_rows = select(hidden, down_hid)
    mixed_part = spread(
        forward_blocks(hidden_rows, down_values[0]), one_hot(down_feat, down_live, feature_count)
    )
    mixed_part = mixed_part.reshape(tok_rows, feature_width)
    upstream_rows = select(upstream, down_feat)
    mixed = lax.psum_scatter(
        mixed_part.astype(jnp.bfloat16), "tensor", scatter_dimension=1, tiled=True
    )
    hidden_grad = spread(
        backward_blocks(upstream_rows, down_values[0]), one_hot(down_hid, down_live, hidden_count)
    )
    gate_delta = (hidden_grad * up_pre * sigma_gate * (1.0 + gate_pre * (1.0 - sigma_gate))).astype(
        jnp.bfloat16
    )
    up_delta = (hidden_grad * activated).astype(jnp.bfloat16)
    gate_delta_rows = select(gate_delta, gate_hid)
    up_delta_rows = select(up_delta, up_hid)
    input_part = spread(
        backward_blocks(gate_delta_rows, gate_values[0]),
        one_hot(gate_feat, gate_live, feature_count),
    )
    input_part = input_part + spread(
        backward_blocks(up_delta_rows, up_values[0]), one_hot(up_feat, up_live, feature_count)
    )
    input_part = input_part.reshape(tok_rows, feature_width)
    gate_term = slot_term(gate_rows, gate_delta_rows, gate_live)
    up_term = slot_term(up_rows, up_delta_rows, up_live)
    down_term = slot_term(hidden_rows, upstream_rows, down_live)
    grad_gate, grad_up, grad_down = (
        lax.psum_scatter(term.astype(jnp.bfloat16), "dp", scatter_dimension=0, tiled=True)
        .astype(jnp.float32)[None]
        for term in (gate_term, up_term, down_term)
    )
    grad_tokens = lax.psum_scatter(
        input_part.astype(jnp.bfloat16), "tensor", scatter_dimension=1, tiled=True
    )
    return (mixed, grad_tokens, grad_gate, grad_up, grad_down)


def solution(mesh):
    in_specs = (
        P("dp", "tensor"),
        P("dp", "tensor"),
        P("tensor", None),
        P("tensor", None, None, None),
        P("tensor", None),
        P("tensor", None, None, None),
        P("tensor", None),
        P("tensor", None, None, None),
    )
    out_specs = (
        P("dp", "tensor"),
        P("dp", "tensor"),
        P("tensor", "dp", None, None),
        P("tensor", "dp", None, None),
        P("tensor", "dp", None, None),
    )
    return jax.shard_map(body, mesh=mesh, in_specs=in_specs, out_specs=out_specs, check_vma=False)
```

```python
import jax
import jax.numpy as jnp
from jax import lax
from jax.sharding import PartitionSpec as P

FF = 14336


def locate(blocks, feature_count):
    flat = blocks[0]
    weight = (flat >= 0).astype(jnp.float32)
    safe = jnp.maximum(flat, 0)
    return (safe // feature_count, safe % feature_count, weight)


def one_hot(targets, weight, count):
    return (targets[:, None] == jnp.arange(count)[None, :]).astype(jnp.float32) * weight[:, None]


def spread(product, table):
    return jnp.einsum("tsn,sc->tcn", product, table, precision=lax.Precision.HIGHEST)


def select(source, position):
    return jnp.take(source, position, axis=1)


def forward_blocks(rows_in, values):
    return jnp.einsum("tsk,skn->tsn", rows_in, values, preferred_element_type=jnp.float32)


def backward_blocks(rows_in, values):
    return jnp.einsum("tsn,skn->tsk", rows_in, values, preferred_element_type=jnp.float32)


def slot_term(left, right, weight):
    product = jnp.einsum("tsk,tsn->skn", left, right, preferred_element_type=jnp.float32)
    return product * weight[:, None, None]


def gather_features(part, axis):
    count = lax.axis_size(axis)
    spread_out = jnp.broadcast_to(part[None], (count,) + part.shape)
    pieces = lax.all_to_all(spread_out, axis, 0, 0, tiled=True)
    return pieces.transpose(1, 0, 2).reshape(part.shape[0], count * part.shape[1])


def scatter_features(full, axis):
    count = lax.axis_size(axis)
    pieces = lax.all_to_all(full.reshape(full.shape[0], count, -1), axis, 1, 1, tiled=True)
    return pieces.astype(jnp.float32).sum(1).astype(jnp.bfloat16)


def body(
    tokens, grad_out, gate_blocks, gate_values, up_blocks, up_values, down_blocks, down_values
):
    gathered_x = gather_features(tokens, "tensor")
    gathered_dy = gather_features(grad_out, "tensor")
    tok_rows, feature_width = gathered_x.shape
    block_size = gate_values.shape[-1]
    feature_count = feature_width // block_size
    hidden_count = FF // (block_size * lax.axis_size("tensor"))
    inputs = gathered_x.reshape(tok_rows, feature_count, block_size)
    upstream = gathered_dy.reshape(tok_rows, feature_count, block_size)
    gate_hid, gate_feat, gate_live = locate(gate_blocks, feature_count)
    up_hid, up_feat, up_live = locate(up_blocks, feature_count)
    down_hid, down_feat, down_live = locate(down_blocks, feature_count)
    gate_rows = select(inputs, gate_feat)
    up_rows = select(inputs, up_feat)
    gate_pre = spread(
        forward_blocks(gate_rows, gate_values[0]), one_hot(gate_hid, gate_live, hidden_count)
    )
    up_pre = spread(forward_blocks(up_rows, up_values[0]), one_hot(up_hid, up_live, hidden_count))
    sigma_gate = jax.nn.sigmoid(gate_pre)
    activated = gate_pre * sigma_gate
    hidden = (activated * up_pre).astype(jnp.bfloat16)
    hidden_rows = select(hidden, down_hid)
    mixed_part = spread(
        forward_blocks(hidden_rows, down_values[0]), one_hot(down_feat, down_live, feature_count)
    )
    mixed_part = mixed_part.reshape(tok_rows, feature_width)
    upstream_rows = select(upstream, down_feat)
    mixed = scatter_features(mixed_part.astype(jnp.bfloat16), "tensor")
    hidden_grad = spread(
        backward_blocks(upstream_rows, down_values[0]), one_hot(down_hid, down_live, hidden_count)
    )
    gate_delta = (hidden_grad * up_pre * sigma_gate * (1.0 + gate_pre * (1.0 - sigma_gate))).astype(
        jnp.bfloat16
    )
    up_delta = (hidden_grad * activated).astype(jnp.bfloat16)
    gate_delta_rows = select(gate_delta, gate_hid)
    up_delta_rows = select(up_delta, up_hid)
    input_part = spread(
        backward_blocks(gate_delta_rows, gate_values[0]),
        one_hot(gate_feat, gate_live, feature_count),
    )
    input_part = input_part + spread(
        backward_blocks(up_delta_rows, up_values[0]), one_hot(up_feat, up_live, feature_count)
    )
    input_part = input_part.reshape(tok_rows, feature_width)
    gate_term = slot_term(gate_rows, gate_delta_rows, gate_live)
    up_term = slot_term(up_rows, up_delta_rows, up_live)
    down_term = slot_term(hidden_rows, upstream_rows, down_live)
    stacked = jnp.stack([gate_term, up_term, down_term], axis=1).astype(jnp.bfloat16)
    combined = lax.all_to_all(stacked, "dp", 0, 0, tiled=True).astype(jnp.float32)
    combined = combined.sum(0, keepdims=True)
    grad_gate = combined[None, :, 0]
    grad_up = combined[None, :, 1]
    grad_down = combined[None, :, 2]
    grad_tokens = scatter_features(input_part.astype(jnp.bfloat16), "tensor")
    return (mixed, grad_tokens, grad_gate, grad_up, grad_down)


def solution(mesh):
    in_specs = (
        P("dp", "tensor"),
        P("dp", "tensor"),
        P("tensor", None),
        P("tensor", None, None, None),
        P("tensor", None),
        P("tensor", None, None, None),
        P("tensor", None),
        P("tensor", None, None, None),
    )
    out_specs = (
        P("dp", "tensor"),
        P("dp", "tensor"),
        P("tensor", "dp", None, None),
        P("tensor", "dp", None, None),
        P("tensor", "dp", None, None),
    )
    return jax.shard_map(body, mesh=mesh, in_specs=in_specs, out_specs=out_specs, check_vma=False)
```

```python
import jax
import jax.numpy as jnp
from jax import lax
from jax.sharding import Mesh
from jax.sharding import PartitionSpec as P

FF = 14336


def locate(blocks, feature_count):
    flat = blocks[0]
    weight = (flat >= 0).astype(jnp.float32)
    safe = jnp.maximum(flat, 0)
    return (safe // feature_count, safe % feature_count, weight)


def one_hot(targets, weight, count):
    return (targets[:, None] == jnp.arange(count)[None, :]).astype(jnp.float32) * weight[:, None]


def spread(product, table):
    return jnp.einsum("tsn,sc->tcn", product, table, precision=lax.Precision.HIGHEST)


def select(source, position):
    return jnp.take(source, position, axis=1)


def forward_blocks(rows_in, values):
    return jnp.einsum("tsk,skn->tsn", rows_in, values, preferred_element_type=jnp.float32)


def backward_blocks(rows_in, values):
    return jnp.einsum("tsn,skn->tsk", rows_in, values, preferred_element_type=jnp.float32)


def slot_term(left, right, weight):
    product = jnp.einsum("tsk,tsn->skn", left, right, preferred_element_type=jnp.float32)
    return product * weight[:, None, None]


def gather_features(parts, axis):
    count = lax.axis_size(axis)
    spread_out = jnp.broadcast_to(parts[None], (count,) + parts.shape)
    pieces = lax.all_to_all(spread_out, axis, 0, 0, tiled=True)
    rows, width = parts.shape[-2:]
    return pieces.transpose(1, 2, 0, 3).reshape(parts.shape[0], rows, count * width)


def reduce_slots(stacked, outer, inner):
    outer_count, inner_count = lax.axis_size(outer), lax.axis_size(inner)
    grid = stacked.reshape((outer_count, inner_count) + stacked.shape[1:])
    grid = lax.all_to_all(grid, inner, 1, 1, tiled=True).astype(jnp.float32).sum(1)
    grid = lax.all_to_all(grid.astype(jnp.bfloat16), outer, 0, 0, tiled=True)
    return grid.astype(jnp.float32).sum(0)


def scatter_features(full, axis):
    count = lax.axis_size(axis)
    pieces = lax.all_to_all(full.reshape(full.shape[0], count, -1), axis, 1, 1, tiled=True)
    return pieces.astype(jnp.float32).sum(1).astype(jnp.bfloat16)


def body(
    tokens, grad_out, gate_blocks, gate_values, up_blocks, up_values, down_blocks, down_values
):
    gathered_x, gathered_dy = gather_features(jnp.stack([tokens, grad_out]), "tensor")
    tok_rows, feature_width = gathered_x.shape
    block_size = gate_values.shape[-1]
    feature_count = feature_width // block_size
    hidden_count = FF // (block_size * lax.axis_size("tensor"))
    inputs = gathered_x.reshape(tok_rows, feature_count, block_size)
    upstream = gathered_dy.reshape(tok_rows, feature_count, block_size)
    gate_hid, gate_feat, gate_live = locate(gate_blocks, feature_count)
    up_hid, up_feat, up_live = locate(up_blocks, feature_count)
    down_hid, down_feat, down_live = locate(down_blocks, feature_count)
    gate_rows = select(inputs, gate_feat)
    up_rows = select(inputs, up_feat)
    gate_pre = spread(
        forward_blocks(gate_rows, gate_values[0]), one_hot(gate_hid, gate_live, hidden_count)
    )
    up_pre = spread(forward_blocks(up_rows, up_values[0]), one_hot(up_hid, up_live, hidden_count))
    sigma_gate = jax.nn.sigmoid(gate_pre)
    activated = gate_pre * sigma_gate
    hidden = (activated * up_pre).astype(jnp.bfloat16)
    hidden_rows = select(hidden, down_hid)
    mixed_part = spread(
        forward_blocks(hidden_rows, down_values[0]), one_hot(down_feat, down_live, feature_count)
    )
    mixed_part = mixed_part.reshape(tok_rows, feature_width)
    upstream_rows = select(upstream, down_feat)
    mixed = scatter_features(mixed_part.astype(jnp.bfloat16), "tensor")
    hidden_grad = spread(
        backward_blocks(upstream_rows, down_values[0]), one_hot(down_hid, down_live, hidden_count)
    )
    gate_delta = (hidden_grad * up_pre * sigma_gate * (1.0 + gate_pre * (1.0 - sigma_gate))).astype(
        jnp.bfloat16
    )
    up_delta = (hidden_grad * activated).astype(jnp.bfloat16)
    gate_delta_rows = select(gate_delta, gate_hid)
    up_delta_rows = select(up_delta, up_hid)
    input_part = spread(
        backward_blocks(gate_delta_rows, gate_values[0]),
        one_hot(gate_feat, gate_live, feature_count),
    )
    input_part = input_part + spread(
        backward_blocks(up_delta_rows, up_values[0]), one_hot(up_feat, up_live, feature_count)
    )
    input_part = input_part.reshape(tok_rows, feature_width)
    gate_term = slot_term(gate_rows, gate_delta_rows, gate_live)
    up_term = slot_term(up_rows, up_delta_rows, up_live)
    down_term = slot_term(hidden_rows, upstream_rows, down_live)
    stacked = jnp.stack([gate_term, up_term, down_term], axis=1).astype(jnp.bfloat16)
    combined = reduce_slots(stacked, "z", "y")[None]
    grad_gate = combined[None, :, 0]
    grad_up = combined[None, :, 1]
    grad_down = combined[None, :, 2]
    grad_tokens = scatter_features(input_part.astype(jnp.bfloat16), "tensor")
    return (mixed, grad_tokens, grad_gate, grad_up, grad_down)


def solution(mesh):
    dp_count, tensor_count = mesh.devices.shape
    y_count = len({device.coords[1] for device in mesh.devices[:, 0]})
    split_mesh = Mesh(
        mesh.devices.reshape(dp_count // y_count, y_count, tensor_count), ("z", "y", "tensor")
    )
    dp = ("z", "y")
    in_specs = (
        P(dp, "tensor"),
        P(dp, "tensor"),
        P("tensor", None),
        P("tensor", None, None, None),
        P("tensor", None),
        P("tensor", None, None, None),
        P("tensor", None),
        P("tensor", None, None, None),
    )
    out_specs = (
        P(dp, "tensor"),
        P(dp, "tensor"),
        P("tensor", dp, None, None),
        P("tensor", dp, None, None),
        P("tensor", dp, None, None),
    )
    return jax.shard_map(
        body, mesh=split_mesh, in_specs=in_specs, out_specs=out_specs, check_vma=False
    )
```

```python
import jax
import jax.numpy as jnp
from jax import lax
from jax.sharding import Mesh
from jax.sharding import PartitionSpec as P

FF = 14336


def locate(blocks, feature_count):
    flat = blocks[0]
    weight = (flat >= 0).astype(jnp.float32)
    safe = jnp.maximum(flat, 0)
    return (safe // feature_count, safe % feature_count, weight)


def one_hot(targets, weight, count):
    return (targets[:, None] == jnp.arange(count)[None, :]).astype(jnp.float32) * weight[:, None]


def spread(product, table):
    return jnp.einsum("tsn,sc->tcn", product, table, precision=lax.Precision.HIGHEST)


def select(source, position):
    return jnp.take(source, position, axis=1)


def forward_blocks(rows_in, values):
    return jnp.einsum("tsk,skn->tsn", rows_in, values, preferred_element_type=jnp.float32)


def backward_blocks(rows_in, values):
    return jnp.einsum("tsn,skn->tsk", rows_in, values, preferred_element_type=jnp.float32)


def slot_term(left, right, weight):
    product = jnp.einsum("tsk,tsn->skn", left, right, preferred_element_type=jnp.float32)
    return product * weight[:, None, None]


def gather_features(parts, axis):
    count = lax.axis_size(axis)
    spread_out = jnp.broadcast_to(parts[None], (count,) + parts.shape)
    pieces = lax.all_to_all(spread_out, axis, 0, 0, tiled=True)
    rows, width = parts.shape[-2:]
    return pieces.transpose(1, 2, 0, 3).reshape(parts.shape[0], rows, count * width)


def reduce_inner(stacked, outer, inner):
    outer_count, inner_count = lax.axis_size(outer), lax.axis_size(inner)
    grid = stacked.reshape((outer_count, inner_count) + stacked.shape[1:])
    grid = lax.all_to_all(grid, inner, 1, 1, tiled=True).astype(jnp.float32).sum(1)
    return grid.astype(jnp.bfloat16)


def reduce_outer(grid, outer):
    grid = lax.all_to_all(grid, outer, 0, 0, tiled=True)
    return grid.astype(jnp.float32).sum(0)


def scatter_features(full, axis):
    count = lax.axis_size(axis)
    own = lax.axis_index(axis)
    pieces = full.reshape(full.shape[0], count, -1).transpose(1, 0, 2)
    total = lax.dynamic_index_in_dim(pieces, own, 0, keepdims=False).astype(jnp.float32)
    for shift in range(1, count):
        outgoing = lax.dynamic_index_in_dim(pieces, (own + shift) % count, 0, keepdims=False)
        pairs = [(source, (source + shift) % count) for source in range(count)]
        total = total + lax.ppermute(outgoing, axis, pairs).astype(jnp.float32)
    return total.astype(jnp.bfloat16)


def body(
    tokens, grad_out, gate_blocks, gate_values, up_blocks, up_values, down_blocks, down_values
):
    gathered_x, gathered_dy = gather_features(jnp.stack([tokens, grad_out]), "tensor")
    tok_rows, feature_width = gathered_x.shape
    block_size = gate_values.shape[-1]
    feature_count = feature_width // block_size
    hidden_count = FF // (block_size * lax.axis_size("tensor"))
    inputs = gathered_x.reshape(tok_rows, feature_count, block_size)
    upstream = gathered_dy.reshape(tok_rows, feature_count, block_size)
    gate_hid, gate_feat, gate_live = locate(gate_blocks, feature_count)
    up_hid, up_feat, up_live = locate(up_blocks, feature_count)
    down_hid, down_feat, down_live = locate(down_blocks, feature_count)
    gate_rows = select(inputs, gate_feat)
    up_rows = select(inputs, up_feat)
    gate_pre = spread(
        forward_blocks(gate_rows, gate_values[0]), one_hot(gate_hid, gate_live, hidden_count)
    )
    up_pre = spread(forward_blocks(up_rows, up_values[0]), one_hot(up_hid, up_live, hidden_count))
    sigma_gate = jax.nn.sigmoid(gate_pre)
    activated = gate_pre * sigma_gate
    hidden = (activated * up_pre).astype(jnp.bfloat16)
    hidden_rows = select(hidden, down_hid)
    upstream_rows = select(upstream, down_feat)
    hidden_grad = spread(
        backward_blocks(upstream_rows, down_values[0]), one_hot(down_hid, down_live, hidden_count)
    )
    gate_delta = (hidden_grad * up_pre * sigma_gate * (1.0 + gate_pre * (1.0 - sigma_gate))).astype(
        jnp.bfloat16
    )
    up_delta = (hidden_grad * activated).astype(jnp.bfloat16)
    gate_delta_rows = select(gate_delta, gate_hid)
    up_delta_rows = select(up_delta, up_hid)
    gate_term = slot_term(gate_rows, gate_delta_rows, gate_live)
    up_term = slot_term(up_rows, up_delta_rows, up_live)
    down_term = slot_term(hidden_rows, upstream_rows, down_live)
    stacked = jnp.stack([gate_term, up_term, down_term], axis=1).astype(jnp.bfloat16)
    stacked, hidden_rows, gate_delta_rows, up_delta_rows = lax.optimization_barrier(
        (stacked, hidden_rows, gate_delta_rows, up_delta_rows)
    )
    partial = reduce_inner(stacked, "z", "y")
    mixed_part = spread(
        forward_blocks(hidden_rows, down_values[0]), one_hot(down_feat, down_live, feature_count)
    )
    mixed_part = mixed_part.reshape(tok_rows, feature_width)
    mixed = scatter_features(mixed_part.astype(jnp.bfloat16), "tensor")
    input_part = spread(
        backward_blocks(gate_delta_rows, gate_values[0]),
        one_hot(gate_feat, gate_live, feature_count),
    )
    input_part = input_part + spread(
        backward_blocks(up_delta_rows, up_values[0]), one_hot(up_feat, up_live, feature_count)
    )
    input_part = input_part.reshape(tok_rows, feature_width)
    grad_tokens = scatter_features(input_part.astype(jnp.bfloat16), "tensor")
    combined = reduce_outer(partial, "z")[None]
    grad_gate = combined[None, :, 0]
    grad_up = combined[None, :, 1]
    grad_down = combined[None, :, 2]
    return (mixed, grad_tokens, grad_gate, grad_up, grad_down)


def solution(mesh):
    dp_count, tensor_count = mesh.devices.shape
    y_count = len({device.coords[1] for device in mesh.devices[:, 0]})
    split_mesh = Mesh(
        mesh.devices.reshape(dp_count // y_count, y_count, tensor_count), ("z", "y", "tensor")
    )
    dp = ("z", "y")
    in_specs = (
        P(dp, "tensor"),
        P(dp, "tensor"),
        P("tensor", None),
        P("tensor", None, None, None),
        P("tensor", None),
        P("tensor", None, None, None),
        P("tensor", None),
        P("tensor", None, None, None),
    )
    out_specs = (
        P(dp, "tensor"),
        P(dp, "tensor"),
        P("tensor", dp, None, None),
        P("tensor", dp, None, None),
        P("tensor", dp, None, None),
    )
    return jax.shard_map(
        body, mesh=split_mesh, in_specs=in_specs, out_specs=out_specs, check_vma=False
    )
```

```python
import jax
import jax.numpy as jnp
from jax import lax
from jax.experimental import pallas as pl
from jax.experimental.pallas import tpu as pltpu
from jax.sharding import Mesh
from jax.sharding import PartitionSpec as P

FF = 14336

NT = (((1,), (1,)), ((), ()))
TN = (((0,), (0,)), ((), ()))


def _dot(a, b, dims=(((1,), (0,)), ((), ()))):
    return lax.dot_general(a, b, dims, preferred_element_type=jnp.float32)


def _front_kernel(gate_at, up_at, down_at, xb, dyb, wg, wu, wd,
                  terms, hid, gdel, udel, gpre, upre, hgrad):
    feature_count = xb.shape[0]
    slots = wg.shape[0]
    gpre[...] = jnp.zeros(gpre.shape, jnp.float32)
    upre[...] = jnp.zeros(upre.shape, jnp.float32)
    hgrad[...] = jnp.zeros(hgrad.shape, jnp.float32)

    @pl.loop(0, slots)
    def _(s):
        bg = gate_at[s]

        @pl.when(bg >= 0)
        def _():
            r, c = bg % feature_count, bg // feature_count
            gpre[c] += _dot(xb[r], wg[s])

        bu = up_at[s]

        @pl.when(bu >= 0)
        def _():
            r, c = bu % feature_count, bu // feature_count
            upre[c] += _dot(xb[r], wu[s])

        bd = down_at[s]

        @pl.when(bd >= 0)
        def _():
            r, c = bd % feature_count, bd // feature_count
            hgrad[c] += _dot(dyb[r], wd[s], NT)

    g = gpre[...]
    u = upre[...]
    hg = hgrad[...]
    sig = 1.0 / (1.0 + jnp.exp(-g))
    act = g * sig
    hid[...] = (act * u).astype(hid.dtype)
    gdel[...] = (hg * u * sig * (1.0 + g * (1.0 - sig))).astype(gdel.dtype)
    udel[...] = (hg * act).astype(udel.dtype)

    @pl.loop(0, slots)
    def _(s):
        bg = gate_at[s]

        @pl.when(bg >= 0)
        def _():
            r, c = bg % feature_count, bg // feature_count
            terms[s, 0] = _dot(xb[r], gdel[c], TN).astype(terms.dtype)

        @pl.when(bg < 0)
        def _():
            terms[s, 0] = jnp.zeros(terms.shape[2:], terms.dtype)

        bu = up_at[s]

        @pl.when(bu >= 0)
        def _():
            r, c = bu % feature_count, bu // feature_count
            terms[s, 1] = _dot(xb[r], udel[c], TN).astype(terms.dtype)

        @pl.when(bu < 0)
        def _():
            terms[s, 1] = jnp.zeros(terms.shape[2:], terms.dtype)

        bd = down_at[s]

        @pl.when(bd >= 0)
        def _():
            r, c = bd % feature_count, bd // feature_count
            terms[s, 2] = _dot(hid[c], dyb[r], TN).astype(terms.dtype)

        @pl.when(bd < 0)
        def _():
            terms[s, 2] = jnp.zeros(terms.shape[2:], terms.dtype)


def _back_kernel(gate_at, up_at, down_at, hid, gdel, udel, wg, wu, wd,
                 mixed, grads, macc, iacc):
    feature_count = mixed.shape[0]
    slots = wg.shape[0]
    macc[...] = jnp.zeros(macc.shape, jnp.float32)
    iacc[...] = jnp.zeros(iacc.shape, jnp.float32)

    @pl.loop(0, slots)
    def _(s):
        bd = down_at[s]

        @pl.when(bd >= 0)
        def _():
            r, c = bd % feature_count, bd // feature_count
            macc[r] += _dot(hid[c], wd[s])

        bg = gate_at[s]

        @pl.when(bg >= 0)
        def _():
            r, c = bg % feature_count, bg // feature_count
            iacc[r] += _dot(gdel[c], wg[s], NT)

        bu = up_at[s]

        @pl.when(bu >= 0)
        def _():
            r, c = bu % feature_count, bu // feature_count
            iacc[r] += _dot(udel[c], wu[s], NT)

    mixed[...] = macc[...].astype(mixed.dtype)
    grads[...] = iacc[...].astype(grads.dtype)


def _specs(n_smem, n_vmem):
    return [pl.BlockSpec(memory_space=pltpu.SMEM)] * n_smem + [
        pl.BlockSpec(memory_space=pltpu.VMEM)
    ] * n_vmem


def front(gate_at, up_at, down_at, xb, dyb, wg, wu, wd, hidden_count, interpret=False):
    feature_count, rows, size = xb.shape
    slots = wg.shape[0]
    hshape = (hidden_count, rows, size)
    return pl.pallas_call(
        _front_kernel,
        out_shape=(
            jax.ShapeDtypeStruct((slots, 3, size, size), jnp.bfloat16),
            jax.ShapeDtypeStruct(hshape, jnp.bfloat16),
            jax.ShapeDtypeStruct(hshape, jnp.bfloat16),
            jax.ShapeDtypeStruct(hshape, jnp.bfloat16),
        ),
        in_specs=_specs(3, 5),
        out_specs=tuple(_specs(0, 4)),
        scratch_shapes=[pltpu.VMEM(hshape, jnp.float32)] * 3,
        interpret=interpret,
    )(gate_at, up_at, down_at, xb, dyb, wg, wu, wd)


def back(gate_at, up_at, down_at, hid, gdel, udel, wg, wu, wd, feature_count, interpret=False):
    _, rows, size = hid.shape
    fshape = (feature_count, rows, size)
    return pl.pallas_call(
        _back_kernel,
        out_shape=(
            jax.ShapeDtypeStruct(fshape, jnp.bfloat16),
            jax.ShapeDtypeStruct(fshape, jnp.bfloat16),
        ),
        in_specs=_specs(3, 6),
        out_specs=tuple(_specs(0, 2)),
        scratch_shapes=[pltpu.VMEM(fshape, jnp.float32)] * 2,
        interpret=interpret,
    )(gate_at, up_at, down_at, hid, gdel, udel, wg, wu, wd)


def gather_blocks(parts, axis, block_size):
    count = lax.axis_size(axis)
    spread_out = jnp.broadcast_to(parts[None], (count,) + parts.shape)
    pieces = lax.all_to_all(spread_out, axis, 0, 0, tiled=True)
    kinds, rows, width = parts.shape
    pieces = pieces.reshape(count, kinds, rows, width // block_size, block_size)
    return pieces.transpose(1, 0, 3, 2, 4).reshape(kinds, -1, rows, block_size)


def scatter_blocks(full, axis):
    count = lax.axis_size(axis)
    own = lax.axis_index(axis)
    pieces = full.reshape((count, -1) + full.shape[1:])
    total = lax.dynamic_index_in_dim(pieces, own, 0, keepdims=False).astype(jnp.float32)
    for shift in range(1, count):
        outgoing = lax.dynamic_index_in_dim(pieces, (own + shift) % count, 0, keepdims=False)
        pairs = [(source, (source + shift) % count) for source in range(count)]
        total = total + lax.ppermute(outgoing, axis, pairs).astype(jnp.float32)
    return total.astype(jnp.bfloat16).transpose(1, 0, 2).reshape(full.shape[1], -1)


def reduce_inner(stacked, outer, inner):
    outer_count, inner_count = lax.axis_size(outer), lax.axis_size(inner)
    grid = stacked.reshape((outer_count, inner_count) + stacked.shape[1:])
    grid = lax.all_to_all(grid, inner, 1, 1, tiled=True).astype(jnp.float32).sum(1)
    return grid.astype(jnp.bfloat16)


def reduce_outer(grid, outer):
    grid = lax.all_to_all(grid, outer, 0, 0, tiled=True)
    return grid.astype(jnp.float32).sum(0)


def body(
    tokens, grad_out, gate_blocks, gate_values, up_blocks, up_values, down_blocks, down_values
):
    block_size = gate_values.shape[-1]
    tensor_count = lax.axis_size("tensor")
    feature_count = tokens.shape[1] * tensor_count // block_size
    hidden_count = FF // (block_size * tensor_count)
    inputs, upstream = gather_blocks(jnp.stack([tokens, grad_out]), "tensor", block_size)
    gate_at, up_at, down_at = gate_blocks[0], up_blocks[0], down_blocks[0]
    weights = (gate_values[0], up_values[0], down_values[0])
    stacked, hidden, gate_delta, up_delta = front(
        gate_at, up_at, down_at, inputs, upstream, *weights, hidden_count
    )
    partial = reduce_inner(stacked, "z", "y")
    mixed_part, input_part = back(
        gate_at, up_at, down_at, hidden, gate_delta, up_delta, *weights, feature_count
    )
    mixed = scatter_blocks(mixed_part, "tensor")
    grad_tokens = scatter_blocks(input_part, "tensor")
    combined = reduce_outer(partial, "z")[None]
    grad_gate = combined[None, :, 0]
    grad_up = combined[None, :, 1]
    grad_down = combined[None, :, 2]
    return (mixed, grad_tokens, grad_gate, grad_up, grad_down)


def solution(mesh):
    dp_count, tensor_count = mesh.devices.shape
    y_count = len({device.coords[1] for device in mesh.devices[:, 0]})
    split_mesh = Mesh(
        mesh.devices.reshape(dp_count // y_count, y_count, tensor_count), ("z", "y", "tensor")
    )
    dp = ("z", "y")
    in_specs = (
        P(dp, "tensor"),
        P(dp, "tensor"),
        P("tensor", None),
        P("tensor", None, None, None),
        P("tensor", None),
        P("tensor", None, None, None),
        P("tensor", None),
        P("tensor", None, None, None),
    )
    out_specs = (
        P(dp, "tensor"),
        P(dp, "tensor"),
        P("tensor", dp, None, None),
        P("tensor", dp, None, None),
        P("tensor", dp, None, None),
    )
    return jax.shard_map(
        body, mesh=split_mesh, in_specs=in_specs, out_specs=out_specs, check_vma=False
    )
```

```python
import jax
import jax.numpy as jnp
from jax import lax
from jax.experimental import pallas as pl
from jax.experimental.pallas import tpu as pltpu
from jax.sharding import Mesh
from jax.sharding import PartitionSpec as P

FF = 14336

NT = (((1,), (1,)), ((), ()))
TN = (((0,), (0,)), ((), ()))


def _dot(a, b, dims=(((1,), (0,)), ((), ()))):
    return lax.dot_general(a, b, dims, preferred_element_type=jnp.float32)


def _front_kernel(gate_at, up_at, down_at, xb, dyb, xt, dyt, wg, wu, wd,
                  terms, hid, gdel, udel, gpre, upre, hgrad):
    feature_count = xb.shape[0]
    slots = wg.shape[0]
    gpre[...] = jnp.zeros(gpre.shape, jnp.float32)
    upre[...] = jnp.zeros(upre.shape, jnp.float32)
    hgrad[...] = jnp.zeros(hgrad.shape, jnp.float32)

    @pl.loop(0, slots)
    def _(s):
        bg = gate_at[s]

        @pl.when(bg >= 0)
        def _():
            r, c = bg % feature_count, bg // feature_count
            gpre[c] += _dot(xb[r], wg[s])

        bu = up_at[s]

        @pl.when(bu >= 0)
        def _():
            r, c = bu % feature_count, bu // feature_count
            upre[c] += _dot(xb[r], wu[s])

        bd = down_at[s]

        @pl.when(bd >= 0)
        def _():
            r, c = bd % feature_count, bd // feature_count
            hgrad[c] += _dot(dyb[r], wd[s], NT)

    g = gpre[...]
    u = upre[...]
    hg = hgrad[...]
    sig = 1.0 / (1.0 + jnp.exp(-g))
    act = g * sig
    hid[...] = (act * u).astype(hid.dtype)
    gdel[...] = (hg * u * sig * (1.0 + g * (1.0 - sig))).astype(gdel.dtype)
    udel[...] = (hg * act).astype(udel.dtype)

    @pl.loop(0, slots)
    def _(s):
        bg = gate_at[s]

        @pl.when(bg >= 0)
        def _():
            r, c = bg % feature_count, bg // feature_count
            terms[s, 0] = _dot(xt[r], gdel[c]).astype(terms.dtype)

        @pl.when(bg < 0)
        def _():
            terms[s, 0] = jnp.zeros(terms.shape[2:], terms.dtype)

        bu = up_at[s]

        @pl.when(bu >= 0)
        def _():
            r, c = bu % feature_count, bu // feature_count
            terms[s, 1] = _dot(xt[r], udel[c]).astype(terms.dtype)

        @pl.when(bu < 0)
        def _():
            terms[s, 1] = jnp.zeros(terms.shape[2:], terms.dtype)

        bd = down_at[s]

        @pl.when(bd >= 0)
        def _():
            r, c = bd % feature_count, bd // feature_count
            terms[s, 2] = _dot(dyt[r], hid[c]).astype(terms.dtype)

        @pl.when(bd < 0)
        def _():
            terms[s, 2] = jnp.zeros(terms.shape[2:], terms.dtype)


def _back_kernel(gate_at, up_at, down_at, hid, gdel, udel, wg, wu, wd,
                 mixed, grads, macc, iacc):
    feature_count = mixed.shape[0]
    slots = wg.shape[0]
    macc[...] = jnp.zeros(macc.shape, jnp.float32)
    iacc[...] = jnp.zeros(iacc.shape, jnp.float32)

    @pl.loop(0, slots)
    def _(s):
        bd = down_at[s]

        @pl.when(bd >= 0)
        def _():
            r, c = bd % feature_count, bd // feature_count
            macc[r] += _dot(hid[c], wd[s])

        bg = gate_at[s]

        @pl.when(bg >= 0)
        def _():
            r, c = bg % feature_count, bg // feature_count
            iacc[r] += _dot(gdel[c], wg[s], NT)

        bu = up_at[s]

        @pl.when(bu >= 0)
        def _():
            r, c = bu % feature_count, bu // feature_count
            iacc[r] += _dot(udel[c], wu[s], NT)

    mixed[...] = macc[...].astype(mixed.dtype)
    grads[...] = iacc[...].astype(grads.dtype)


def _specs(n_smem, n_vmem):
    return [pl.BlockSpec(memory_space=pltpu.SMEM)] * n_smem + [
        pl.BlockSpec(memory_space=pltpu.VMEM)
    ] * n_vmem


def front(gate_at, up_at, down_at, xb, dyb, xt, dyt, wg, wu, wd, hidden_count, interpret=False):
    feature_count, rows, size = xb.shape
    slots = wg.shape[0]
    hshape = (hidden_count, rows, size)
    return pl.pallas_call(
        _front_kernel,
        out_shape=(
            jax.ShapeDtypeStruct((slots, 3, size, size), jnp.bfloat16),
            jax.ShapeDtypeStruct(hshape, jnp.bfloat16),
            jax.ShapeDtypeStruct(hshape, jnp.bfloat16),
            jax.ShapeDtypeStruct(hshape, jnp.bfloat16),
        ),
        in_specs=_specs(3, 7),
        out_specs=tuple(_specs(0, 4)),
        scratch_shapes=[pltpu.VMEM(hshape, jnp.float32)] * 3,
        cost_estimate=pl.CostEstimate(
            flops=6 * slots * 2 * size**3,
            transcendentals=hidden_count * rows * size,
            bytes_accessed=(4 * feature_count * rows + 6 * slots * size + 3 * hidden_count * rows)
            * size * 2,
        ),
        interpret=interpret,
    )(gate_at, up_at, down_at, xb, dyb, xt, dyt, wg, wu, wd)


def back(gate_at, up_at, down_at, hid, gdel, udel, wg, wu, wd, feature_count, interpret=False):
    _, rows, size = hid.shape
    fshape = (feature_count, rows, size)
    return pl.pallas_call(
        _back_kernel,
        out_shape=(
            jax.ShapeDtypeStruct(fshape, jnp.bfloat16),
            jax.ShapeDtypeStruct(fshape, jnp.bfloat16),
        ),
        in_specs=_specs(3, 6),
        out_specs=tuple(_specs(0, 2)),
        scratch_shapes=[pltpu.VMEM(fshape, jnp.float32)] * 2,
        cost_estimate=pl.CostEstimate(
            flops=3 * wg.shape[0] * 2 * size**3,
            transcendentals=0,
            bytes_accessed=(3 * hid.shape[0] * rows + 3 * wg.shape[0] * size + 2 * feature_count * rows)
            * size * 2,
        ),
        interpret=interpret,
    )(gate_at, up_at, down_at, hid, gdel, udel, wg, wu, wd)


def gather_blocks(parts, axis, block_size):
    count = lax.axis_size(axis)
    spread_out = jnp.broadcast_to(parts[None], (count,) + parts.shape)
    pieces = lax.all_to_all(spread_out, axis, 0, 0, tiled=True)
    kinds, rows, width = parts.shape
    pieces = pieces.reshape(count, kinds, rows, width // block_size, block_size)
    blocks = pieces.transpose(1, 0, 3, 2, 4).reshape(kinds, -1, rows, block_size)
    flipped = pieces.transpose(1, 0, 3, 4, 2).reshape(kinds, -1, block_size, rows)
    return blocks, flipped


def scatter_blocks(full, axis):
    count = lax.axis_size(axis)
    own = lax.axis_index(axis)
    pieces = full.reshape((count, -1) + full.shape[1:])
    total = lax.dynamic_index_in_dim(pieces, own, 0, keepdims=False).astype(jnp.float32)
    for shift in range(1, count):
        outgoing = lax.dynamic_index_in_dim(pieces, (own + shift) % count, 0, keepdims=False)
        pairs = [(source, (source + shift) % count) for source in range(count)]
        total = total + lax.ppermute(outgoing, axis, pairs).astype(jnp.float32)
    return total.astype(jnp.bfloat16).transpose(1, 0, 2).reshape(full.shape[1], -1)


def reduce_inner(stacked, outer, inner):
    outer_count, inner_count = lax.axis_size(outer), lax.axis_size(inner)
    grid = stacked.reshape((outer_count, inner_count) + stacked.shape[1:])
    grid = lax.all_to_all(grid, inner, 1, 1, tiled=True).astype(jnp.float32).sum(1)
    return grid.astype(jnp.bfloat16)


def reduce_outer(grid, outer):
    grid = lax.all_to_all(grid, outer, 0, 0, tiled=True)
    return grid.astype(jnp.float32).sum(0)


def body(
    tokens, grad_out, gate_blocks, gate_values, up_blocks, up_values, down_blocks, down_values
):
    block_size = gate_values.shape[-1]
    tensor_count = lax.axis_size("tensor")
    feature_count = tokens.shape[1] * tensor_count // block_size
    hidden_count = FF // (block_size * tensor_count)
    (inputs, upstream), (inputs_t, upstream_t) = gather_blocks(
        jnp.stack([tokens, grad_out]), "tensor", block_size
    )
    gate_at, up_at, down_at = gate_blocks[0], up_blocks[0], down_blocks[0]
    weights = (gate_values[0], up_values[0], down_values[0])
    stacked, hidden, gate_delta, up_delta = front(
        gate_at, up_at, down_at, inputs, upstream, inputs_t, upstream_t, *weights, hidden_count
    )
    partial = reduce_inner(stacked, "z", "y")
    mixed_part, input_part = back(
        gate_at, up_at, down_at, hidden, gate_delta, up_delta, *weights, feature_count
    )
    mixed = scatter_blocks(mixed_part, "tensor")
    grad_tokens = scatter_blocks(input_part, "tensor")
    combined = reduce_outer(partial, "z")[None]
    grad_gate = combined[None, :, 0]
    grad_up = combined[None, :, 1]
    grad_down = combined[None, :, 2].swapaxes(-1, -2)
    return (mixed, grad_tokens, grad_gate, grad_up, grad_down)


def solution(mesh):
    dp_count, tensor_count = mesh.devices.shape
    y_count = len({device.coords[1] for device in mesh.devices[:, 0]})
    split_mesh = Mesh(
        mesh.devices.reshape(dp_count // y_count, y_count, tensor_count), ("z", "y", "tensor")
    )
    dp = ("z", "y")
    in_specs = (
        P(dp, "tensor"),
        P(dp, "tensor"),
        P("tensor", None),
        P("tensor", None, None, None),
        P("tensor", None),
        P("tensor", None, None, None),
        P("tensor", None),
        P("tensor", None, None, None),
    )
    out_specs = (
        P(dp, "tensor"),
        P(dp, "tensor"),
        P("tensor", dp, None, None),
        P("tensor", dp, None, None),
        P("tensor", dp, None, None),
    )
    return jax.shard_map(
        body, mesh=split_mesh, in_specs=in_specs, out_specs=out_specs, check_vma=False
    )
```

```python
import jax
import jax.numpy as jnp
from jax import lax
from jax.experimental import pallas as pl
from jax.experimental.pallas import tpu as pltpu
from jax.sharding import Mesh
from jax.sharding import PartitionSpec as P

FF = 14336

NT = (((1,), (1,)), ((), ()))


def _dot(a, b, dims=(((1,), (0,)), ((), ()))):
    return lax.dot_general(a, b, dims, preferred_element_type=jnp.float32)


def _front_kernel(gate_at, up_at, down_at, xb, dyb, xt, dyt, wg, wu, wd,
                  terms, hid, gdel, udel, gpre, upre, hgrad):
    inner = terms.shape[0]
    feature_count = xb.shape[0]
    slots = wg.shape[0]
    gpre[...] = jnp.zeros(gpre.shape, jnp.float32)
    upre[...] = jnp.zeros(upre.shape, jnp.float32)
    hgrad[...] = jnp.zeros(hgrad.shape, jnp.float32)

    @pl.loop(0, slots)
    def _(s):
        bg = gate_at[s]

        @pl.when(bg >= 0)
        def _():
            r, c = bg % feature_count, bg // feature_count
            gpre[c] += _dot(xb[r], wg[s])

        bu = up_at[s]

        @pl.when(bu >= 0)
        def _():
            r, c = bu % feature_count, bu // feature_count
            upre[c] += _dot(xb[r], wu[s])

        bd = down_at[s]

        @pl.when(bd >= 0)
        def _():
            r, c = bd % feature_count, bd // feature_count
            hgrad[c] += _dot(dyb[r], wd[s], NT)

    g = gpre[...]
    u = upre[...]
    hg = hgrad[...]
    sig = 1.0 / (1.0 + jnp.exp(-g))
    act = g * sig
    hid[...] = (act * u).astype(hid.dtype)
    gdel[...] = (hg * u * sig * (1.0 + g * (1.0 - sig))).astype(gdel.dtype)
    udel[...] = (hg * act).astype(udel.dtype)

    @pl.loop(0, slots)
    def _(s):
        bg = gate_at[s]

        @pl.when(bg >= 0)
        def _():
            r, c = bg % feature_count, bg // feature_count
            terms[s % inner, s // inner, 0] = _dot(xt[r], gdel[c]).astype(terms.dtype)

        @pl.when(bg < 0)
        def _():
            terms[s % inner, s // inner, 0] = jnp.zeros(terms.shape[3:], terms.dtype)

        bu = up_at[s]

        @pl.when(bu >= 0)
        def _():
            r, c = bu % feature_count, bu // feature_count
            terms[s % inner, s // inner, 1] = _dot(xt[r], udel[c]).astype(terms.dtype)

        @pl.when(bu < 0)
        def _():
            terms[s % inner, s // inner, 1] = jnp.zeros(terms.shape[3:], terms.dtype)

        bd = down_at[s]

        @pl.when(bd >= 0)
        def _():
            r, c = bd % feature_count, bd // feature_count
            terms[s % inner, s // inner, 2] = _dot(dyt[r], hid[c]).astype(terms.dtype)

        @pl.when(bd < 0)
        def _():
            terms[s % inner, s // inner, 2] = jnp.zeros(terms.shape[3:], terms.dtype)


def _back_kernel(gate_at, up_at, down_at, hid, gdel, udel, wg, wu, wd,
                 mixed, grads, macc, iacc):
    feature_count = mixed.shape[0]
    slots = wg.shape[0]
    macc[...] = jnp.zeros(macc.shape, jnp.float32)
    iacc[...] = jnp.zeros(iacc.shape, jnp.float32)

    @pl.loop(0, slots)
    def _(s):
        bd = down_at[s]

        @pl.when(bd >= 0)
        def _():
            r, c = bd % feature_count, bd // feature_count
            macc[r] += _dot(hid[c], wd[s])

        bg = gate_at[s]

        @pl.when(bg >= 0)
        def _():
            r, c = bg % feature_count, bg // feature_count
            iacc[r] += _dot(gdel[c], wg[s], NT)

        bu = up_at[s]

        @pl.when(bu >= 0)
        def _():
            r, c = bu % feature_count, bu // feature_count
            iacc[r] += _dot(udel[c], wu[s], NT)

    mixed[...] = macc[...].astype(mixed.dtype)
    grads[...] = iacc[...].astype(grads.dtype)


def _specs(n_smem, n_vmem):
    return [pl.BlockSpec(memory_space=pltpu.SMEM)] * n_smem + [
        pl.BlockSpec(memory_space=pltpu.VMEM)
    ] * n_vmem


def front(gate_at, up_at, down_at, xb, dyb, xt, dyt, wg, wu, wd, hidden_count, inner,
          interpret=False):
    feature_count, rows, size = xb.shape
    slots = wg.shape[0]
    hshape = (hidden_count, rows, size)
    return pl.pallas_call(
        _front_kernel,
        out_shape=(
            jax.ShapeDtypeStruct((inner, slots // inner, 3, size, size), jnp.bfloat16),
            jax.ShapeDtypeStruct(hshape, jnp.bfloat16),
            jax.ShapeDtypeStruct(hshape, jnp.bfloat16),
            jax.ShapeDtypeStruct(hshape, jnp.bfloat16),
        ),
        in_specs=_specs(3, 7),
        out_specs=tuple(_specs(0, 4)),
        scratch_shapes=[pltpu.VMEM(hshape, jnp.float32)] * 3,
        cost_estimate=pl.CostEstimate(
            flops=6 * slots * 2 * size**3,
            transcendentals=hidden_count * rows * size,
            bytes_accessed=(4 * feature_count * rows + 6 * slots * size + 3 * hidden_count * rows)
            * size * 2,
        ),
        interpret=interpret,
    )(gate_at, up_at, down_at, xb, dyb, xt, dyt, wg, wu, wd)


def back(gate_at, up_at, down_at, hid, gdel, udel, wg, wu, wd, feature_count, interpret=False):
    _, rows, size = hid.shape
    fshape = (feature_count, rows, size)
    return pl.pallas_call(
        _back_kernel,
        out_shape=(
            jax.ShapeDtypeStruct(fshape, jnp.bfloat16),
            jax.ShapeDtypeStruct(fshape, jnp.bfloat16),
        ),
        in_specs=_specs(3, 6),
        out_specs=tuple(_specs(0, 2)),
        scratch_shapes=[pltpu.VMEM(fshape, jnp.float32)] * 2,
        cost_estimate=pl.CostEstimate(
            flops=3 * wg.shape[0] * 2 * size**3,
            transcendentals=0,
            bytes_accessed=(3 * hid.shape[0] * rows + 3 * wg.shape[0] * size + 2 * feature_count * rows)
            * size * 2,
        ),
        interpret=interpret,
    )(gate_at, up_at, down_at, hid, gdel, udel, wg, wu, wd)


def gather_blocks(parts, axis, block_size):
    count = lax.axis_size(axis)
    spread_out = jnp.broadcast_to(parts[None], (count,) + parts.shape)
    pieces = lax.all_to_all(spread_out, axis, 0, 0, tiled=True)
    kinds, rows, width = parts.shape
    pieces = pieces.reshape(count, kinds, rows, width // block_size, block_size)
    blocks = pieces.transpose(1, 0, 3, 2, 4).reshape(kinds, -1, rows, block_size)
    flipped = pieces.transpose(1, 0, 3, 4, 2).reshape(kinds, -1, block_size, rows)
    return blocks, flipped


def scatter_blocks(full, axis):
    count = lax.axis_size(axis)
    own = lax.axis_index(axis)
    pieces = full.reshape((count, -1) + full.shape[1:])
    total = lax.dynamic_index_in_dim(pieces, own, 0, keepdims=False).astype(jnp.float32)
    for shift in range(1, count):
        outgoing = lax.dynamic_index_in_dim(pieces, (own + shift) % count, 0, keepdims=False)
        pairs = [(source, (source + shift) % count) for source in range(count)]
        total = total + lax.ppermute(outgoing, axis, pairs).astype(jnp.float32)
    return total.astype(jnp.bfloat16).transpose(1, 0, 2).reshape(full.shape[1], -1)


def reduce_inner(grid, inner):
    count = lax.axis_size(inner)
    own = lax.axis_index(inner)
    total = lax.dynamic_index_in_dim(grid, own, 0, keepdims=False).astype(jnp.float32)
    for shift in range(1, count):
        outgoing = lax.dynamic_index_in_dim(grid, (own + shift) % count, 0, keepdims=False)
        pairs = [(source, (source + shift) % count) for source in range(count)]
        total = total + lax.ppermute(outgoing, inner, pairs).astype(jnp.float32)
    return total.astype(jnp.bfloat16)


def reduce_outer(grid, outer):
    grid = lax.all_to_all(grid, outer, 0, 0, tiled=True)
    return grid.astype(jnp.float32).sum(0)


def layer(
    tokens, grad_out, gate_blocks, gate_values, up_blocks, up_values, down_blocks, down_values
):
    block_size = gate_values.shape[-1]
    tensor_count = lax.axis_size("tensor")
    feature_count = tokens.shape[1] * tensor_count // block_size
    hidden_count = FF // (block_size * tensor_count)
    (inputs, upstream), (inputs_t, upstream_t) = gather_blocks(
        jnp.stack([tokens, grad_out]), "tensor", block_size
    )
    gate_at, up_at, down_at = gate_blocks[0], up_blocks[0], down_blocks[0]
    weights = (gate_values[0], up_values[0], down_values[0])
    stacked, hidden, gate_delta, up_delta = front(
        gate_at, up_at, down_at, inputs, upstream, inputs_t, upstream_t, *weights, hidden_count,
        lax.axis_size("y"),
    )
    partial = reduce_inner(stacked, "y")
    mixed_part, input_part = back(
        gate_at, up_at, down_at, hidden, gate_delta, up_delta, *weights, feature_count
    )
    mixed = scatter_blocks(mixed_part, "tensor")
    grad_tokens = scatter_blocks(input_part, "tensor")
    combined = reduce_outer(partial, "z")[None]
    grad_gate = combined[None, :, 0]
    grad_up = combined[None, :, 1]
    grad_down = combined[None, :, 2].swapaxes(-1, -2)
    return (mixed, grad_tokens, grad_gate, grad_up, grad_down)


def solution(mesh):
    dp_count, tensor_count = mesh.devices.shape
    y_count = len({device.coords[1] for device in mesh.devices[:, 0]})
    split_mesh = Mesh(
        mesh.devices.reshape(dp_count // y_count, y_count, tensor_count), ("z", "y", "tensor")
    )
    dp = ("z", "y")
    in_specs = (
        P(dp, "tensor"),
        P(dp, "tensor"),
        P("tensor", None),
        P("tensor", None, None, None),
        P("tensor", None),
        P("tensor", None, None, None),
        P("tensor", None),
        P("tensor", None, None, None),
    )
    out_specs = (
        P(dp, "tensor"),
        P(dp, "tensor"),
        P("tensor", dp, None, None),
        P("tensor", dp, None, None),
        P("tensor", dp, None, None),
    )
    return jax.shard_map(
        layer, mesh=split_mesh, in_specs=in_specs, out_specs=out_specs, check_vma=False
    )
```

```python
import jax
import jax.numpy as jnp
from jax import lax
from jax.experimental import pallas as pl
from jax.experimental.pallas import tpu as pltpu
from jax.sharding import Mesh
from jax.sharding import PartitionSpec as P

FF = 14336

NT = (((1,), (1,)), ((), ()))


def _dot(a, b, dims=(((1,), (0,)), ((), ()))):
    return lax.dot_general(a, b, dims, preferred_element_type=jnp.float32)


def _front_kernel(gate_at, up_at, down_at, xb, dyb, xt, dyt, wg, wu, wd,
                  terms, hid, gdel, udel, gpre, upre, hgrad):
    inner = terms.shape[0]
    feature_count = xb.shape[0]
    slots = wg.shape[0]
    gpre[...] = jnp.zeros(gpre.shape, jnp.float32)
    upre[...] = jnp.zeros(upre.shape, jnp.float32)
    hgrad[...] = jnp.zeros(hgrad.shape, jnp.float32)

    @pl.loop(0, slots)
    def _(s):
        bg = gate_at[s]

        @pl.when(bg >= 0)
        def _():
            r, c = bg % feature_count, bg // feature_count
            gpre[c] += _dot(xb[r], wg[s])

        bu = up_at[s]

        @pl.when(bu >= 0)
        def _():
            r, c = bu % feature_count, bu // feature_count
            upre[c] += _dot(xb[r], wu[s])

        bd = down_at[s]

        @pl.when(bd >= 0)
        def _():
            r, c = bd % feature_count, bd // feature_count
            hgrad[c] += _dot(dyb[r], wd[s], NT)

    g = gpre[...]
    u = upre[...]
    hg = hgrad[...]
    sig = 1.0 / (1.0 + jnp.exp(-g))
    act = g * sig
    hid[...] = (act * u).astype(hid.dtype)
    gdel[...] = (hg * u * sig * (1.0 + g * (1.0 - sig))).astype(gdel.dtype)
    udel[...] = (hg * act).astype(udel.dtype)

    @pl.loop(0, slots)
    def _(s):
        bg = gate_at[s]

        @pl.when(bg >= 0)
        def _():
            r, c = bg % feature_count, bg // feature_count
            terms[s % inner, s // inner, 0] = _dot(xt[r], gdel[c]).astype(terms.dtype)

        @pl.when(bg < 0)
        def _():
            terms[s % inner, s // inner, 0] = jnp.zeros(terms.shape[3:], terms.dtype)

        bu = up_at[s]

        @pl.when(bu >= 0)
        def _():
            r, c = bu % feature_count, bu // feature_count
            terms[s % inner, s // inner, 1] = _dot(xt[r], udel[c]).astype(terms.dtype)

        @pl.when(bu < 0)
        def _():
            terms[s % inner, s // inner, 1] = jnp.zeros(terms.shape[3:], terms.dtype)

        bd = down_at[s]

        @pl.when(bd >= 0)
        def _():
            r, c = bd % feature_count, bd // feature_count
            terms[s % inner, s // inner, 2] = _dot(dyt[r], hid[c]).astype(terms.dtype)

        @pl.when(bd < 0)
        def _():
            terms[s % inner, s // inner, 2] = jnp.zeros(terms.shape[3:], terms.dtype)


def _back_kernel(gate_at, up_at, down_at, hid, gdel, udel, wg, wu, wd,
                 mixed, grads, macc, iacc):
    feature_count = mixed.shape[0]
    slots = wg.shape[0]
    macc[...] = jnp.zeros(macc.shape, jnp.float32)
    iacc[...] = jnp.zeros(iacc.shape, jnp.float32)

    @pl.loop(0, slots)
    def _(s):
        bd = down_at[s]

        @pl.when(bd >= 0)
        def _():
            r, c = bd % feature_count, bd // feature_count
            macc[r] += _dot(hid[c], wd[s])

        bg = gate_at[s]

        @pl.when(bg >= 0)
        def _():
            r, c = bg % feature_count, bg // feature_count
            iacc[r] += _dot(gdel[c], wg[s], NT)

        bu = up_at[s]

        @pl.when(bu >= 0)
        def _():
            r, c = bu % feature_count, bu // feature_count
            iacc[r] += _dot(udel[c], wu[s], NT)

    mixed[...] = macc[...].astype(mixed.dtype)
    grads[...] = iacc[...].astype(grads.dtype)


def _specs(n_smem, n_vmem):
    return [pl.BlockSpec(memory_space=pltpu.SMEM)] * n_smem + [
        pl.BlockSpec(memory_space=pltpu.VMEM)
    ] * n_vmem


def front(gate_at, up_at, down_at, xb, dyb, xt, dyt, wg, wu, wd, hidden_count, inner,
          interpret=False):
    feature_count, rows, size = xb.shape
    slots = wg.shape[0]
    hshape = (hidden_count, rows, size)
    return pl.pallas_call(
        _front_kernel,
        out_shape=(
            jax.ShapeDtypeStruct((inner, slots // inner, 3, size, size), jnp.bfloat16),
            jax.ShapeDtypeStruct(hshape, jnp.bfloat16),
            jax.ShapeDtypeStruct(hshape, jnp.bfloat16),
            jax.ShapeDtypeStruct(hshape, jnp.bfloat16),
        ),
        in_specs=_specs(3, 7),
        out_specs=tuple(_specs(0, 4)),
        scratch_shapes=[pltpu.VMEM(hshape, jnp.float32)] * 3,
        cost_estimate=pl.CostEstimate(
            flops=6 * slots * 2 * size**3,
            transcendentals=hidden_count * rows * size,
            bytes_accessed=(4 * feature_count * rows + 6 * slots * size + 3 * hidden_count * rows)
            * size * 2,
        ),
        interpret=interpret,
    )(gate_at, up_at, down_at, xb, dyb, xt, dyt, wg, wu, wd)


def back(gate_at, up_at, down_at, hid, gdel, udel, wg, wu, wd, feature_count, interpret=False):
    _, rows, size = hid.shape
    fshape = (feature_count, rows, size)
    return pl.pallas_call(
        _back_kernel,
        out_shape=(
            jax.ShapeDtypeStruct(fshape, jnp.bfloat16),
            jax.ShapeDtypeStruct(fshape, jnp.bfloat16),
        ),
        in_specs=_specs(3, 6),
        out_specs=tuple(_specs(0, 2)),
        scratch_shapes=[pltpu.VMEM(fshape, jnp.float32)] * 2,
        cost_estimate=pl.CostEstimate(
            flops=3 * wg.shape[0] * 2 * size**3,
            transcendentals=0,
            bytes_accessed=(3 * hid.shape[0] * rows + 3 * wg.shape[0] * size + 2 * feature_count * rows)
            * size * 2,
        ),
        interpret=interpret,
    )(gate_at, up_at, down_at, hid, gdel, udel, wg, wu, wd)


def gather_blocks(parts, axis, block_size):
    count = lax.axis_size(axis)
    spread_out = jnp.broadcast_to(parts[None], (count,) + parts.shape)
    pieces = lax.all_to_all(spread_out, axis, 0, 0, tiled=True)
    kinds, rows, width = parts.shape
    pieces = pieces.reshape(count, kinds, rows, width // block_size, block_size)
    blocks = pieces.transpose(1, 0, 3, 2, 4).reshape(kinds, -1, rows, block_size)
    flipped = pieces.transpose(1, 0, 3, 4, 2).reshape(kinds, -1, block_size, rows)
    return blocks, flipped


def scatter_blocks(full, axis):
    count = lax.axis_size(axis)
    own = lax.axis_index(axis)
    pieces = full.reshape((count, -1) + full.shape[1:])
    total = lax.dynamic_index_in_dim(pieces, own, 0, keepdims=False).astype(jnp.float32)
    for shift in range(1, count):
        outgoing = lax.dynamic_index_in_dim(pieces, (own + shift) % count, 0, keepdims=False)
        pairs = [(source, (source + shift) % count) for source in range(count)]
        total = total + lax.ppermute(outgoing, axis, pairs).astype(jnp.float32)
    return total.astype(jnp.bfloat16).transpose(1, 0, 2).reshape(full.shape[1], -1)


def reduce_inner(grid, inner):
    count = lax.axis_size(inner)
    own = lax.axis_index(inner)
    total = lax.dynamic_index_in_dim(grid, own, 0, keepdims=False).astype(jnp.float32)
    for shift in range(1, count):
        outgoing = lax.dynamic_index_in_dim(grid, (own + shift) % count, 0, keepdims=False)
        pairs = [(source, (source + shift) % count) for source in range(count)]
        total = total + lax.ppermute(outgoing, inner, pairs).astype(jnp.float32)
    return total.astype(jnp.bfloat16)


def reduce_outer(grid, outer):
    grid = lax.all_to_all(grid, outer, 0, 0, tiled=True)
    return grid.astype(jnp.float32).sum(0)


def layer(
    tokens, grad_out, gate_blocks, gate_values, up_blocks, up_values, down_blocks, down_values
):
    block_size = gate_values.shape[-1]
    tensor_count = lax.axis_size("tensor")
    feature_count = tokens.shape[1] * tensor_count // block_size
    hidden_count = FF // (block_size * tensor_count)
    (inputs, upstream), (inputs_t, upstream_t) = gather_blocks(
        jnp.stack([tokens, grad_out]), "tensor", block_size
    )
    gate_at, up_at, down_at = gate_blocks[0], up_blocks[0], down_blocks[0]
    weights = (gate_values[0], up_values[0], down_values[0])
    stacked, hidden, gate_delta, up_delta = front(
        gate_at, up_at, down_at, inputs, upstream, inputs_t, upstream_t, *weights, hidden_count,
        lax.axis_size("y"),
    )
    half = stacked.shape[-2] // 2
    partial = reduce_inner(stacked[..., :half, :], "y")
    later = reduce_inner(stacked[..., half:, :], "y")
    mixed_part, input_part = back(
        gate_at, up_at, down_at, hidden, gate_delta, up_delta, *weights, feature_count
    )
    mixed = scatter_blocks(mixed_part, "tensor")
    grad_tokens = scatter_blocks(input_part, "tensor")
    combined = reduce_outer(partial, "z")
    combined = jnp.concatenate([combined, reduce_outer(later, "z")], axis=-2)[None]
    grad_gate = combined[None, :, 0]
    grad_up = combined[None, :, 1]
    grad_down = combined[None, :, 2].swapaxes(-1, -2)
    return (mixed, grad_tokens, grad_gate, grad_up, grad_down)


def solution(mesh):
    dp_count, tensor_count = mesh.devices.shape
    y_count = len({device.coords[1] for device in mesh.devices[:, 0]})
    split_mesh = Mesh(
        mesh.devices.reshape(dp_count // y_count, y_count, tensor_count), ("z", "y", "tensor")
    )
    dp = ("z", "y")
    in_specs = (
        P(dp, "tensor"),
        P(dp, "tensor"),
        P("tensor", None),
        P("tensor", None, None, None),
        P("tensor", None),
        P("tensor", None, None, None),
        P("tensor", None),
        P("tensor", None, None, None),
    )
    out_specs = (
        P(dp, "tensor"),
        P(dp, "tensor"),
        P("tensor", dp, None, None),
        P("tensor", dp, None, None),
        P("tensor", dp, None, None),
    )
    return jax.shard_map(
        layer, mesh=split_mesh, in_specs=in_specs, out_specs=out_specs, check_vma=False
    )
```

```python
import jax
import jax.numpy as jnp
from jax import lax
from jax.experimental import pallas as pl
from jax.experimental.pallas import tpu as pltpu
from jax.sharding import Mesh
from jax.sharding import PartitionSpec as P

FF = 14336

NT = (((1,), (1,)), ((), ()))


def _dot(a, b, dims=(((1,), (0,)), ((), ()))):
    return lax.dot_general(a, b, dims, preferred_element_type=jnp.float32)


def _front_kernel(turn, gate_at, up_at, down_at, xb, dyb, xt, dyt, wg, wu, wd,
                  terms, hid, gdel, udel, gpre, upre, hgrad):
    inner = terms.shape[0]
    own = turn[0]
    feature_count = xb.shape[0]
    slots = wg.shape[0]
    gpre[...] = jnp.zeros(gpre.shape, jnp.float32)
    upre[...] = jnp.zeros(upre.shape, jnp.float32)
    hgrad[...] = jnp.zeros(hgrad.shape, jnp.float32)

    @pl.loop(0, slots)
    def _(s):
        bg = gate_at[s]

        @pl.when(bg >= 0)
        def _():
            r, c = bg % feature_count, bg // feature_count
            gpre[c] += _dot(xb[r], wg[s])

        bu = up_at[s]

        @pl.when(bu >= 0)
        def _():
            r, c = bu % feature_count, bu // feature_count
            upre[c] += _dot(xb[r], wu[s])

        bd = down_at[s]

        @pl.when(bd >= 0)
        def _():
            r, c = bd % feature_count, bd // feature_count
            hgrad[c] += _dot(dyb[r], wd[s], NT)

    g = gpre[...]
    u = upre[...]
    hg = hgrad[...]
    sig = 1.0 / (1.0 + jnp.exp(-g))
    act = g * sig
    hid[...] = (act * u).astype(hid.dtype)
    gdel[...] = (hg * u * sig * (1.0 + g * (1.0 - sig))).astype(gdel.dtype)
    udel[...] = (hg * act).astype(udel.dtype)

    @pl.loop(0, slots)
    def _(s):
        bg = gate_at[s]

        @pl.when(bg >= 0)
        def _():
            r, c = bg % feature_count, bg // feature_count
            terms[(s % inner + inner - own) % inner, s // inner, 0] = _dot(xt[r], gdel[c]).astype(terms.dtype)

        @pl.when(bg < 0)
        def _():
            terms[(s % inner + inner - own) % inner, s // inner, 0] = jnp.zeros(terms.shape[3:], terms.dtype)

        bu = up_at[s]

        @pl.when(bu >= 0)
        def _():
            r, c = bu % feature_count, bu // feature_count
            terms[(s % inner + inner - own) % inner, s // inner, 1] = _dot(xt[r], udel[c]).astype(terms.dtype)

        @pl.when(bu < 0)
        def _():
            terms[(s % inner + inner - own) % inner, s // inner, 1] = jnp.zeros(terms.shape[3:], terms.dtype)

        bd = down_at[s]

        @pl.when(bd >= 0)
        def _():
            r, c = bd % feature_count, bd // feature_count
            terms[(s % inner + inner - own) % inner, s // inner, 2] = _dot(dyt[r], hid[c]).astype(terms.dtype)

        @pl.when(bd < 0)
        def _():
            terms[(s % inner + inner - own) % inner, s // inner, 2] = jnp.zeros(terms.shape[3:], terms.dtype)


def _back_kernel(turn, gate_at, up_at, down_at, hid, gdel, udel, wg, wu, wd,
                 mixed, grads, macc, iacc):
    feature_count = macc.shape[0]
    slots = wg.shape[0]
    macc[...] = jnp.zeros(macc.shape, jnp.float32)
    iacc[...] = jnp.zeros(iacc.shape, jnp.float32)

    @pl.loop(0, slots)
    def _(s):
        bd = down_at[s]

        @pl.when(bd >= 0)
        def _():
            r, c = bd % feature_count, bd // feature_count
            macc[r] += _dot(hid[c], wd[s])

        bg = gate_at[s]

        @pl.when(bg >= 0)
        def _():
            r, c = bg % feature_count, bg // feature_count
            iacc[r] += _dot(gdel[c], wg[s], NT)

        bu = up_at[s]

        @pl.when(bu >= 0)
        def _():
            r, c = bu % feature_count, bu // feature_count
            iacc[r] += _dot(udel[c], wu[s], NT)

    count, per = mixed.shape[:2]
    for piece in range(count):
        at = (piece + count - turn[0]) % count
        mixed[at] = macc[piece * per:(piece + 1) * per].astype(mixed.dtype)
        grads[at] = iacc[piece * per:(piece + 1) * per].astype(grads.dtype)


def _specs(n_smem, n_vmem):
    return [pl.BlockSpec(memory_space=pltpu.SMEM)] * n_smem + [
        pl.BlockSpec(memory_space=pltpu.VMEM)
    ] * n_vmem


def front(turn, gate_at, up_at, down_at, xb, dyb, xt, dyt, wg, wu, wd, hidden_count, inner,
          interpret=False):
    feature_count, rows, size = xb.shape
    slots = wg.shape[0]
    hshape = (hidden_count, rows, size)
    return pl.pallas_call(
        _front_kernel,
        out_shape=(
            jax.ShapeDtypeStruct((inner, slots // inner, 3, size, size), jnp.bfloat16),
            jax.ShapeDtypeStruct(hshape, jnp.bfloat16),
            jax.ShapeDtypeStruct(hshape, jnp.bfloat16),
            jax.ShapeDtypeStruct(hshape, jnp.bfloat16),
        ),
        in_specs=_specs(4, 7),
        out_specs=tuple(_specs(0, 4)),
        scratch_shapes=[pltpu.VMEM(hshape, jnp.float32)] * 3,
        cost_estimate=pl.CostEstimate(
            flops=6 * slots * 2 * size**3,
            transcendentals=hidden_count * rows * size,
            bytes_accessed=(4 * feature_count * rows + 6 * slots * size + 3 * hidden_count * rows)
            * size * 2,
        ),
        interpret=interpret,
    )(turn, gate_at, up_at, down_at, xb, dyb, xt, dyt, wg, wu, wd)


def back(turn, gate_at, up_at, down_at, hid, gdel, udel, wg, wu, wd, feature_count, count,
         interpret=False):
    _, rows, size = hid.shape
    fshape = (feature_count, rows, size)
    pshape = (count, feature_count // count, rows, size)
    return pl.pallas_call(
        _back_kernel,
        out_shape=(
            jax.ShapeDtypeStruct(pshape, jnp.bfloat16),
            jax.ShapeDtypeStruct(pshape, jnp.bfloat16),
        ),
        in_specs=_specs(4, 6),
        out_specs=tuple(_specs(0, 2)),
        scratch_shapes=[pltpu.VMEM(fshape, jnp.float32)] * 2,
        cost_estimate=pl.CostEstimate(
            flops=3 * wg.shape[0] * 2 * size**3,
            transcendentals=0,
            bytes_accessed=(3 * hid.shape[0] * rows + 3 * wg.shape[0] * size + 2 * feature_count * rows)
            * size * 2,
        ),
        interpret=interpret,
    )(turn, gate_at, up_at, down_at, hid, gdel, udel, wg, wu, wd)


def gather_blocks(parts, axis, block_size):
    count = lax.axis_size(axis)
    spread_out = jnp.broadcast_to(parts[None], (count,) + parts.shape)
    pieces = lax.all_to_all(spread_out, axis, 0, 0, tiled=True)
    kinds, rows, width = parts.shape
    pieces = pieces.reshape(count, kinds, rows, width // block_size, block_size)
    blocks = pieces.transpose(1, 0, 3, 2, 4).reshape(kinds, -1, rows, block_size)
    flipped = pieces.transpose(1, 0, 3, 4, 2).reshape(kinds, -1, block_size, rows)
    return blocks, flipped


def scatter_blocks(pieces, axis):
    count = pieces.shape[0]
    total = pieces[0].astype(jnp.float32)
    for shift in range(1, count):
        pairs = [(source, (source + shift) % count) for source in range(count)]
        total = total + lax.ppermute(pieces[shift], axis, pairs).astype(jnp.float32)
    return total.astype(jnp.bfloat16).transpose(1, 0, 2).reshape(pieces.shape[2], -1)


def reduce_inner(grid, inner):
    count = grid.shape[0]
    total = grid[0].astype(jnp.float32)
    for shift in range(1, count):
        pairs = [(source, (source + shift) % count) for source in range(count)]
        total = total + lax.ppermute(grid[shift], inner, pairs).astype(jnp.float32)
    return total.astype(jnp.bfloat16)


def reduce_outer(grid, outer):
    grid = lax.all_to_all(grid, outer, 0, 0, tiled=True)
    return grid.astype(jnp.float32).sum(0)


def layer(
    tokens, grad_out, gate_blocks, gate_values, up_blocks, up_values, down_blocks, down_values
):
    block_size = gate_values.shape[-1]
    tensor_count = lax.axis_size("tensor")
    feature_count = tokens.shape[1] * tensor_count // block_size
    hidden_count = FF // (block_size * tensor_count)
    (inputs, upstream), (inputs_t, upstream_t) = gather_blocks(
        jnp.stack([tokens, grad_out]), "tensor", block_size
    )
    gate_at, up_at, down_at = gate_blocks[0], up_blocks[0], down_blocks[0]
    weights = (gate_values[0], up_values[0], down_values[0])
    y_turn = lax.axis_index("y").astype(jnp.int32).reshape(1)
    tensor_turn = lax.axis_index("tensor").astype(jnp.int32).reshape(1)
    stacked, hidden, gate_delta, up_delta = front(
        y_turn, gate_at, up_at, down_at, inputs, upstream, inputs_t, upstream_t, *weights, hidden_count,
        lax.axis_size("y"),
    )
    partial = reduce_inner(stacked, "y")
    mixed_part, input_part = back(
        tensor_turn, gate_at, up_at, down_at, hidden, gate_delta, up_delta, *weights,
        feature_count, tensor_count,
    )
    mixed = scatter_blocks(mixed_part, "tensor")
    grad_tokens = scatter_blocks(input_part, "tensor")
    combined = reduce_outer(partial, "z")[None]
    grad_gate = combined[None, :, 0]
    grad_up = combined[None, :, 1]
    grad_down = combined[None, :, 2].swapaxes(-1, -2)
    return (mixed, grad_tokens, grad_gate, grad_up, grad_down)


def solution(mesh):
    dp_count, tensor_count = mesh.devices.shape
    y_count = len({device.coords[1] for device in mesh.devices[:, 0]})
    split_mesh = Mesh(
        mesh.devices.reshape(dp_count // y_count, y_count, tensor_count), ("z", "y", "tensor")
    )
    dp = ("z", "y")
    in_specs = (
        P(dp, "tensor"),
        P(dp, "tensor"),
        P("tensor", None),
        P("tensor", None, None, None),
        P("tensor", None),
        P("tensor", None, None, None),
        P("tensor", None),
        P("tensor", None, None, None),
    )
    out_specs = (
        P(dp, "tensor"),
        P(dp, "tensor"),
        P("tensor", dp, None, None),
        P("tensor", dp, None, None),
        P("tensor", dp, None, None),
    )
    return jax.shard_map(layer, mesh=split_mesh, in_specs=in_specs, out_specs=out_specs, check_vma=False)
```

```python
import jax
import jax.numpy as jnp
from jax import lax
from jax.experimental import pallas as pl
from jax.experimental.pallas import tpu as pltpu
from jax.sharding import Mesh
from jax.sharding import PartitionSpec as P

FF = 14336

NT = (((1,), (1,)), ((), ()))


def _dot(a, b, dims=(((1,), (0,)), ((), ()))):
    return lax.dot_general(a, b, dims, preferred_element_type=jnp.float32)


def _front_kernel(gate_at, up_at, down_at, xb, dyb, xt, dyt, wg, wu, wd,
                  terms, hid, gdel, udel, gpre, upre, hgrad):
    inner = terms.shape[0]
    feature_count = xb.shape[0]
    slots = wg.shape[0]
    gpre[...] = jnp.zeros(gpre.shape, jnp.float32)
    upre[...] = jnp.zeros(upre.shape, jnp.float32)
    hgrad[...] = jnp.zeros(hgrad.shape, jnp.float32)

    @pl.loop(0, slots)
    def _(s):
        bg = gate_at[s]

        @pl.when(bg >= 0)
        def _():
            r, c = bg % feature_count, bg // feature_count
            gpre[c] += _dot(xb[r], wg[s])

        bu = up_at[s]

        @pl.when(bu >= 0)
        def _():
            r, c = bu % feature_count, bu // feature_count
            upre[c] += _dot(xb[r], wu[s])

        bd = down_at[s]

        @pl.when(bd >= 0)
        def _():
            r, c = bd % feature_count, bd // feature_count
            hgrad[c] += _dot(dyb[r], wd[s], NT)

    g = gpre[...]
    u = upre[...]
    hg = hgrad[...]
    sig = 1.0 / (1.0 + jnp.exp(-g))
    act = g * sig
    hid[...] = (act * u).astype(hid.dtype)
    gdel[...] = (hg * u * sig * (1.0 + g * (1.0 - sig))).astype(gdel.dtype)
    udel[...] = (hg * act).astype(udel.dtype)

    @pl.loop(0, slots)
    def _(s):
        bg = gate_at[s]

        @pl.when(bg >= 0)
        def _():
            r, c = bg % feature_count, bg // feature_count
            terms[s % inner, s // inner, 0] = _dot(xt[r], gdel[c]).astype(terms.dtype)

        @pl.when(bg < 0)
        def _():
            terms[s % inner, s // inner, 0] = jnp.zeros(terms.shape[3:], terms.dtype)

        bu = up_at[s]

        @pl.when(bu >= 0)
        def _():
            r, c = bu % feature_count, bu // feature_count
            terms[s % inner, s // inner, 1] = _dot(xt[r], udel[c]).astype(terms.dtype)

        @pl.when(bu < 0)
        def _():
            terms[s % inner, s // inner, 1] = jnp.zeros(terms.shape[3:], terms.dtype)

        bd = down_at[s]

        @pl.when(bd >= 0)
        def _():
            r, c = bd % feature_count, bd // feature_count
            terms[s % inner, s // inner, 2] = _dot(dyt[r], hid[c]).astype(terms.dtype)

        @pl.when(bd < 0)
        def _():
            terms[s % inner, s // inner, 2] = jnp.zeros(terms.shape[3:], terms.dtype)


def _back_kernel(gate_at, up_at, down_at, hid, gdel, udel, wg, wu, wd,
                 mixed, grads, macc, iacc):
    feature_count = mixed.shape[0]
    slots = wg.shape[0]
    macc[...] = jnp.zeros(macc.shape, jnp.float32)
    iacc[...] = jnp.zeros(iacc.shape, jnp.float32)

    @pl.loop(0, slots)
    def _(s):
        bd = down_at[s]

        @pl.when(bd >= 0)
        def _():
            r, c = bd % feature_count, bd // feature_count
            macc[r] += _dot(hid[c], wd[s])

        bg = gate_at[s]

        @pl.when(bg >= 0)
        def _():
            r, c = bg % feature_count, bg // feature_count
            iacc[r] += _dot(gdel[c], wg[s], NT)

        bu = up_at[s]

        @pl.when(bu >= 0)
        def _():
            r, c = bu % feature_count, bu // feature_count
            iacc[r] += _dot(udel[c], wu[s], NT)

    mixed[...] = macc[...].astype(mixed.dtype)
    grads[...] = iacc[...].astype(grads.dtype)


def _specs(n_smem, n_vmem):
    return [pl.BlockSpec(memory_space=pltpu.SMEM)] * n_smem + [
        pl.BlockSpec(memory_space=pltpu.VMEM)
    ] * n_vmem


def front(gate_at, up_at, down_at, xb, dyb, xt, dyt, wg, wu, wd, hidden_count, inner,
          interpret=False):
    feature_count, rows, size = xb.shape
    slots = wg.shape[0]
    hshape = (hidden_count, rows, size)
    return pl.pallas_call(
        _front_kernel,
        out_shape=(
            jax.ShapeDtypeStruct((inner, slots // inner, 3, size, size), jnp.bfloat16),
            jax.ShapeDtypeStruct(hshape, jnp.bfloat16),
            jax.ShapeDtypeStruct(hshape, jnp.bfloat16),
            jax.ShapeDtypeStruct(hshape, jnp.bfloat16),
        ),
        in_specs=_specs(3, 7),
        out_specs=tuple(_specs(0, 4)),
        scratch_shapes=[pltpu.VMEM(hshape, jnp.float32)] * 3,
        cost_estimate=pl.CostEstimate(
            flops=6 * slots * 2 * size**3,
            transcendentals=hidden_count * rows * size,
            bytes_accessed=(4 * feature_count * rows + 6 * slots * size + 3 * hidden_count * rows)
            * size * 2,
        ),
        interpret=interpret,
    )(gate_at, up_at, down_at, xb, dyb, xt, dyt, wg, wu, wd)


def back(gate_at, up_at, down_at, hid, gdel, udel, wg, wu, wd, feature_count, interpret=False):
    _, rows, size = hid.shape
    fshape = (feature_count, rows, size)
    return pl.pallas_call(
        _back_kernel,
        out_shape=(
            jax.ShapeDtypeStruct(fshape, jnp.bfloat16),
            jax.ShapeDtypeStruct(fshape, jnp.bfloat16),
        ),
        in_specs=_specs(3, 6),
        out_specs=tuple(_specs(0, 2)),
        scratch_shapes=[pltpu.VMEM(fshape, jnp.float32)] * 2,
        cost_estimate=pl.CostEstimate(
            flops=3 * wg.shape[0] * 2 * size**3,
            transcendentals=0,
            bytes_accessed=(3 * hid.shape[0] * rows + 3 * wg.shape[0] * size + 2 * feature_count * rows)
            * size * 2,
        ),
        interpret=interpret,
    )(gate_at, up_at, down_at, hid, gdel, udel, wg, wu, wd)


def gather_blocks(parts, axis, block_size):
    count = lax.axis_size(axis)
    spread_out = jnp.broadcast_to(parts[None], (count,) + parts.shape)
    pieces = lax.all_to_all(spread_out, axis, 0, 0, tiled=True)
    kinds, rows, width = parts.shape
    pieces = pieces.reshape(count, kinds, rows, width // block_size, block_size)
    blocks = pieces.transpose(1, 0, 3, 2, 4).reshape(kinds, -1, rows, block_size)
    flipped = pieces.transpose(1, 0, 3, 4, 2).reshape(kinds, -1, block_size, rows)
    return blocks, flipped


def scatter_blocks(full, axis):
    count = lax.axis_size(axis)
    own = lax.axis_index(axis)
    pieces = full.reshape((count, -1) + full.shape[1:])
    total = lax.dynamic_index_in_dim(pieces, own, 0, keepdims=False).astype(jnp.float32)
    for shift in range(1, count):
        outgoing = lax.dynamic_index_in_dim(pieces, (own + shift) % count, 0, keepdims=False)
        pairs = [(source, (source + shift) % count) for source in range(count)]
        total = total + lax.ppermute(outgoing, axis, pairs).astype(jnp.float32)
    return total.astype(jnp.bfloat16).transpose(1, 0, 2).reshape(full.shape[1], -1)


def reduce_inner(grid, inner):
    count = lax.axis_size(inner)
    own = lax.axis_index(inner)
    total = lax.dynamic_index_in_dim(grid, own, 0, keepdims=False).astype(jnp.float32)
    for shift in range(1, count):
        outgoing = lax.dynamic_index_in_dim(grid, (own + shift) % count, 0, keepdims=False)
        pairs = [(source, (source + shift) % count) for source in range(count)]
        total = total + lax.ppermute(outgoing, inner, pairs).astype(jnp.float32)
    return total.astype(jnp.bfloat16)


def reduce_outer(grid, outer):
    count = lax.axis_size(outer)
    own = lax.axis_index(outer)
    total = lax.dynamic_index_in_dim(grid, own, 0, keepdims=False).astype(jnp.float32)
    for shift in range(1, count):
        outgoing = lax.dynamic_index_in_dim(grid, (own + shift) % count, 0, keepdims=False)
        pairs = [(source, (source + shift) % count) for source in range(count)]
        total = total + lax.ppermute(outgoing, outer, pairs).astype(jnp.float32)
    return total


def layer(
    tokens, grad_out, gate_blocks, gate_values, up_blocks, up_values, down_blocks, down_values
):
    block_size = gate_values.shape[-1]
    tensor_count = lax.axis_size("tensor")
    feature_count = tokens.shape[1] * tensor_count // block_size
    hidden_count = FF // (block_size * tensor_count)
    (inputs, upstream), (inputs_t, upstream_t) = gather_blocks(
        jnp.stack([tokens, grad_out]), "tensor", block_size
    )
    gate_at, up_at, down_at = gate_blocks[0], up_blocks[0], down_blocks[0]
    weights = (gate_values[0], up_values[0], down_values[0])
    stacked, hidden, gate_delta, up_delta = front(
        gate_at, up_at, down_at, inputs, upstream, inputs_t, upstream_t, *weights, hidden_count,
        lax.axis_size("y"),
    )
    partial = reduce_inner(stacked, "y")
    mixed_part, input_part = back(
        gate_at, up_at, down_at, hidden, gate_delta, up_delta, *weights, feature_count
    )
    mixed = scatter_blocks(mixed_part, "tensor")
    grad_tokens = scatter_blocks(input_part, "tensor")
    combined = reduce_outer(partial, "z")[None]
    grad_gate = combined[None, :, 0]
    grad_up = combined[None, :, 1]
    grad_down = combined[None, :, 2].swapaxes(-1, -2)
    return (mixed, grad_tokens, grad_gate, grad_up, grad_down)


def solution(mesh):
    dp_count, tensor_count = mesh.devices.shape
    y_count = len({device.coords[1] for device in mesh.devices[:, 0]})
    split_mesh = Mesh(
        mesh.devices.reshape(dp_count // y_count, y_count, tensor_count), ("z", "y", "tensor")
    )
    dp = ("z", "y")
    in_specs = (
        P(dp, "tensor"),
        P(dp, "tensor"),
        P("tensor", None),
        P("tensor", None, None, None),
        P("tensor", None),
        P("tensor", None, None, None),
        P("tensor", None),
        P("tensor", None, None, None),
    )
    out_specs = (
        P(dp, "tensor"),
        P(dp, "tensor"),
        P("tensor", dp, None, None),
        P("tensor", dp, None, None),
        P("tensor", dp, None, None),
    )
    return jax.shard_map(
        layer, mesh=split_mesh, in_specs=in_specs, out_specs=out_specs, check_vma=False
    )
```

```python
import jax
import jax.numpy as jnp
from jax import lax
from jax.experimental import pallas as pl
from jax.experimental.pallas import tpu as pltpu
from jax.sharding import Mesh
from jax.sharding import PartitionSpec as P

FF = 14336

NT = (((1,), (1,)), ((), ()))


def _dot(a, b, dims=(((1,), (0,)), ((), ()))):
    return lax.dot_general(a, b, dims, preferred_element_type=jnp.float32)


def _front_kernel(gate_at, up_at, down_at, xb, dyb, xt, dyt, wg, wu, wd,
                  terms, hid, gdel, udel, gpre, upre, hgrad):
    inner = terms.shape[0]
    feature_count = xb.shape[0]
    slots = wg.shape[0]
    gpre[...] = jnp.zeros(gpre.shape, jnp.float32)
    upre[...] = jnp.zeros(upre.shape, jnp.float32)
    hgrad[...] = jnp.zeros(hgrad.shape, jnp.float32)

    @pl.loop(0, slots)
    def _(s):
        bg = gate_at[s]

        @pl.when(bg >= 0)
        def _():
            r, c = bg % feature_count, bg // feature_count
            gpre[c] += _dot(xb[r], wg[s])

        bu = up_at[s]

        @pl.when(bu >= 0)
        def _():
            r, c = bu % feature_count, bu // feature_count
            upre[c] += _dot(xb[r], wu[s])

        bd = down_at[s]

        @pl.when(bd >= 0)
        def _():
            r, c = bd % feature_count, bd // feature_count
            hgrad[c] += _dot(dyb[r], wd[s], NT)

    g = gpre[...]
    u = upre[...]
    hg = hgrad[...]
    sig = 1.0 / (1.0 + jnp.exp(-g))
    act = g * sig
    hid[...] = (act * u).astype(hid.dtype)
    gdel[...] = (hg * u * sig * (1.0 + g * (1.0 - sig))).astype(gdel.dtype)
    udel[...] = (hg * act).astype(udel.dtype)

    @pl.loop(0, slots)
    def _(s):
        bg = gate_at[s]

        @pl.when(bg >= 0)
        def _():
            r, c = bg % feature_count, bg // feature_count
            terms[s % inner, s // inner, 0] = _dot(xt[r], gdel[c]).astype(terms.dtype)

        @pl.when(bg < 0)
        def _():
            terms[s % inner, s // inner, 0] = jnp.zeros(terms.shape[3:], terms.dtype)

        bu = up_at[s]

        @pl.when(bu >= 0)
        def _():
            r, c = bu % feature_count, bu // feature_count
            terms[s % inner, s // inner, 1] = _dot(xt[r], udel[c]).astype(terms.dtype)

        @pl.when(bu < 0)
        def _():
            terms[s % inner, s // inner, 1] = jnp.zeros(terms.shape[3:], terms.dtype)

        bd = down_at[s]

        @pl.when(bd >= 0)
        def _():
            r, c = bd % feature_count, bd // feature_count
            terms[s % inner, s // inner, 2] = _dot(dyt[r], hid[c]).astype(terms.dtype)

        @pl.when(bd < 0)
        def _():
            terms[s % inner, s // inner, 2] = jnp.zeros(terms.shape[3:], terms.dtype)


def _back_kernel(gate_at, up_at, down_at, hid, gdel, udel, wg, wu, wd,
                 mixed, grads, macc, iacc):
    feature_count = mixed.shape[0]
    slots = wg.shape[0]
    macc[...] = jnp.zeros(macc.shape, jnp.float32)
    iacc[...] = jnp.zeros(iacc.shape, jnp.float32)

    @pl.loop(0, slots)
    def _(s):
        bd = down_at[s]

        @pl.when(bd >= 0)
        def _():
            r, c = bd % feature_count, bd // feature_count
            macc[r] += _dot(hid[c], wd[s])

        bg = gate_at[s]

        @pl.when(bg >= 0)
        def _():
            r, c = bg % feature_count, bg // feature_count
            iacc[r] += _dot(gdel[c], wg[s], NT)

        bu = up_at[s]

        @pl.when(bu >= 0)
        def _():
            r, c = bu % feature_count, bu // feature_count
            iacc[r] += _dot(udel[c], wu[s], NT)

    mixed[...] = macc[...].astype(mixed.dtype)
    grads[...] = iacc[...].astype(grads.dtype)


def _specs(n_smem, n_vmem):
    return [pl.BlockSpec(memory_space=pltpu.SMEM)] * n_smem + [
        pl.BlockSpec(memory_space=pltpu.VMEM)
    ] * n_vmem


def front(gate_at, up_at, down_at, xb, dyb, xt, dyt, wg, wu, wd, hidden_count, inner,
          interpret=False):
    feature_count, rows, size = xb.shape
    slots = wg.shape[0]
    hshape = (hidden_count, rows, size)
    return pl.pallas_call(
        _front_kernel,
        out_shape=(
            jax.ShapeDtypeStruct((inner, slots // inner, 3, size, size), jnp.bfloat16),
            jax.ShapeDtypeStruct(hshape, jnp.bfloat16),
            jax.ShapeDtypeStruct(hshape, jnp.bfloat16),
            jax.ShapeDtypeStruct(hshape, jnp.bfloat16),
        ),
        in_specs=_specs(3, 7),
        out_specs=tuple(_specs(0, 4)),
        scratch_shapes=[pltpu.VMEM(hshape, jnp.float32)] * 3,
        cost_estimate=pl.CostEstimate(
            flops=6 * slots * 2 * size**3,
            transcendentals=hidden_count * rows * size,
            bytes_accessed=(4 * feature_count * rows + 6 * slots * size + 3 * hidden_count * rows)
            * size * 2,
        ),
        interpret=interpret,
    )(gate_at, up_at, down_at, xb, dyb, xt, dyt, wg, wu, wd)


def back(gate_at, up_at, down_at, hid, gdel, udel, wg, wu, wd, feature_count, interpret=False):
    _, rows, size = hid.shape
    fshape = (feature_count, rows, size)
    return pl.pallas_call(
        _back_kernel,
        out_shape=(
            jax.ShapeDtypeStruct(fshape, jnp.bfloat16),
            jax.ShapeDtypeStruct(fshape, jnp.bfloat16),
        ),
        in_specs=_specs(3, 6),
        out_specs=tuple(_specs(0, 2)),
        scratch_shapes=[pltpu.VMEM(fshape, jnp.float32)] * 2,
        cost_estimate=pl.CostEstimate(
            flops=3 * wg.shape[0] * 2 * size**3,
            transcendentals=0,
            bytes_accessed=(3 * hid.shape[0] * rows + 3 * wg.shape[0] * size + 2 * feature_count * rows)
            * size * 2,
        ),
        interpret=interpret,
    )(gate_at, up_at, down_at, hid, gdel, udel, wg, wu, wd)


def gather_blocks(parts, axis, block_size):
    count = lax.axis_size(axis)
    spread_out = jnp.broadcast_to(parts[None], (count,) + parts.shape)
    pieces = lax.all_to_all(spread_out, axis, 0, 0, tiled=True)
    kinds, rows, width = parts.shape
    pieces = pieces.reshape(count, kinds, rows, width // block_size, block_size)
    blocks = pieces.transpose(1, 0, 3, 2, 4).reshape(kinds, -1, rows, block_size)
    flipped = pieces.transpose(1, 0, 3, 4, 2).reshape(kinds, -1, block_size, rows)
    return blocks, flipped


def scatter_blocks(fulls, axis):
    count = lax.axis_size(axis)
    own = lax.axis_index(axis)
    rows = fulls[0].shape[1]
    pieces = jnp.stack([full.reshape((count, -1) + full.shape[1:]) for full in fulls], 1)
    total = lax.dynamic_index_in_dim(pieces, own, 0, keepdims=False).astype(jnp.float32)
    for shift in range(1, count):
        outgoing = lax.dynamic_index_in_dim(pieces, (own + shift) % count, 0, keepdims=False)
        pairs = [(source, (source + shift) % count) for source in range(count)]
        total = total + lax.ppermute(outgoing, axis, pairs).astype(jnp.float32)
    total = total.astype(jnp.bfloat16)
    return [part.transpose(1, 0, 2).reshape(rows, -1) for part in total]


def reduce_inner(grid, inner):
    count = lax.axis_size(inner)
    own = lax.axis_index(inner)
    total = lax.dynamic_index_in_dim(grid, own, 0, keepdims=False).astype(jnp.float32)
    for shift in range(1, count):
        outgoing = lax.dynamic_index_in_dim(grid, (own + shift) % count, 0, keepdims=False)
        pairs = [(source, (source + shift) % count) for source in range(count)]
        total = total + lax.ppermute(outgoing, inner, pairs).astype(jnp.float32)
    return total.astype(jnp.bfloat16)


def reduce_outer(grid, outer):
    count = lax.axis_size(outer)
    own = lax.axis_index(outer)
    total = lax.dynamic_index_in_dim(grid, own, 0, keepdims=False).astype(jnp.float32)
    for shift in range(1, count):
        outgoing = lax.dynamic_index_in_dim(grid, (own + shift) % count, 0, keepdims=False)
        pairs = [(source, (source + shift) % count) for source in range(count)]
        total = total + lax.ppermute(outgoing, outer, pairs).astype(jnp.float32)
    return total


def layer(
    tokens, grad_out, gate_blocks, gate_values, up_blocks, up_values, down_blocks, down_values
):
    block_size = gate_values.shape[-1]
    tensor_count = lax.axis_size("tensor")
    feature_count = tokens.shape[1] * tensor_count // block_size
    hidden_count = FF // (block_size * tensor_count)
    (inputs, upstream), (inputs_t, upstream_t) = gather_blocks(
        jnp.stack([tokens, grad_out]), "tensor", block_size
    )
    gate_at, up_at, down_at = gate_blocks[0], up_blocks[0], down_blocks[0]
    weights = (gate_values[0], up_values[0], down_values[0])
    stacked, hidden, gate_delta, up_delta = front(
        gate_at, up_at, down_at, inputs, upstream, inputs_t, upstream_t, *weights, hidden_count,
        lax.axis_size("y"),
    )
    partial = reduce_inner(stacked, "y")
    mixed_part, input_part = back(
        gate_at, up_at, down_at, hidden, gate_delta, up_delta, *weights, feature_count
    )
    mixed, grad_tokens = scatter_blocks((mixed_part, input_part), "tensor")
    combined = reduce_outer(partial, "z")[None]
    grad_gate = combined[None, :, 0]
    grad_up = combined[None, :, 1]
    grad_down = combined[None, :, 2].swapaxes(-1, -2)
    return (mixed, grad_tokens, grad_gate, grad_up, grad_down)


def solution(mesh):
    dp_count, tensor_count = mesh.devices.shape
    y_count = len({device.coords[1] for device in mesh.devices[:, 0]})
    split_mesh = Mesh(
        mesh.devices.reshape(dp_count // y_count, y_count, tensor_count), ("z", "y", "tensor")
    )
    dp = ("z", "y")
    in_specs = (
        P(dp, "tensor"),
        P(dp, "tensor"),
        P("tensor", None),
        P("tensor", None, None, None),
        P("tensor", None),
        P("tensor", None, None, None),
        P("tensor", None),
        P("tensor", None, None, None),
    )
    out_specs = (
        P(dp, "tensor"),
        P(dp, "tensor"),
        P("tensor", dp, None, None),
        P("tensor", dp, None, None),
        P("tensor", dp, None, None),
    )
    return jax.shard_map(
        layer, mesh=split_mesh, in_specs=in_specs, out_specs=out_specs, check_vma=False
    )
```

```python
import jax
import jax.numpy as jnp
from jax import lax
from jax.experimental import pallas as pl
from jax.experimental.pallas import tpu as pltpu
from jax.sharding import Mesh
from jax.sharding import PartitionSpec as P

FF = 14336

NT = (((1,), (1,)), ((), ()))


def _dot(a, b, dims=(((1,), (0,)), ((), ()))):
    return lax.dot_general(a, b, dims, preferred_element_type=jnp.float32)


def _front_kernel(gate_at, up_at, down_at, xb, dyb, xt, dyt, wg, wu, wd,
                  terms, hid, gdel, udel, gpre, upre, hgrad):
    inner = terms.shape[0]
    feature_count = xb.shape[0]
    slots = wg.shape[0]
    gpre[...] = jnp.zeros(gpre.shape, jnp.float32)
    upre[...] = jnp.zeros(upre.shape, jnp.float32)
    hgrad[...] = jnp.zeros(hgrad.shape, jnp.float32)

    @pl.loop(0, slots)
    def _(s):
        bg = gate_at[s]

        @pl.when(bg >= 0)
        def _():
            r, c = bg % feature_count, bg // feature_count
            gpre[c] += _dot(xb[r], wg[s])

        bu = up_at[s]

        @pl.when(bu >= 0)
        def _():
            r, c = bu % feature_count, bu // feature_count
            upre[c] += _dot(xb[r], wu[s])

        bd = down_at[s]

        @pl.when(bd >= 0)
        def _():
            r, c = bd % feature_count, bd // feature_count
            hgrad[c] += _dot(dyb[r], wd[s], NT)

    g = gpre[...]
    u = upre[...]
    hg = hgrad[...]
    sig = 1.0 / (1.0 + jnp.exp(-g))
    act = g * sig
    hid[...] = (act * u).astype(hid.dtype)
    gdel[...] = (hg * u * sig * (1.0 + g * (1.0 - sig))).astype(gdel.dtype)
    udel[...] = (hg * act).astype(udel.dtype)

    @pl.loop(0, slots)
    def _(s):
        bg = gate_at[s]

        @pl.when(bg >= 0)
        def _():
            r, c = bg % feature_count, bg // feature_count
            terms[s % inner, s // inner, 0] = _dot(xt[r], gdel[c]).astype(terms.dtype)

        @pl.when(bg < 0)
        def _():
            terms[s % inner, s // inner, 0] = jnp.zeros(terms.shape[3:], terms.dtype)

        bu = up_at[s]

        @pl.when(bu >= 0)
        def _():
            r, c = bu % feature_count, bu // feature_count
            terms[s % inner, s // inner, 1] = _dot(xt[r], udel[c]).astype(terms.dtype)

        @pl.when(bu < 0)
        def _():
            terms[s % inner, s // inner, 1] = jnp.zeros(terms.shape[3:], terms.dtype)

        bd = down_at[s]

        @pl.when(bd >= 0)
        def _():
            r, c = bd % feature_count, bd // feature_count
            terms[s % inner, s // inner, 2] = _dot(dyt[r], hid[c]).astype(terms.dtype)

        @pl.when(bd < 0)
        def _():
            terms[s % inner, s // inner, 2] = jnp.zeros(terms.shape[3:], terms.dtype)


def _back_kernel(gate_at, up_at, down_at, hid, gdel, udel, wg, wu, wd,
                 mixed, grads, macc, iacc):
    feature_count = mixed.shape[0]
    slots = wg.shape[0]
    macc[...] = jnp.zeros(macc.shape, jnp.float32)
    iacc[...] = jnp.zeros(iacc.shape, jnp.float32)

    @pl.loop(0, slots)
    def _(s):
        bd = down_at[s]

        @pl.when(bd >= 0)
        def _():
            r, c = bd % feature_count, bd // feature_count
            macc[r] += _dot(hid[c], wd[s])

        bg = gate_at[s]

        @pl.when(bg >= 0)
        def _():
            r, c = bg % feature_count, bg // feature_count
            iacc[r] += _dot(gdel[c], wg[s], NT)

        bu = up_at[s]

        @pl.when(bu >= 0)
        def _():
            r, c = bu % feature_count, bu // feature_count
            iacc[r] += _dot(udel[c], wu[s], NT)

    mixed[...] = macc[...].astype(mixed.dtype)
    grads[...] = iacc[...].astype(grads.dtype)


def _specs(n_smem, n_vmem):
    return [pl.BlockSpec(memory_space=pltpu.SMEM)] * n_smem + [
        pl.BlockSpec(memory_space=pltpu.VMEM)
    ] * n_vmem


def front(gate_at, up_at, down_at, xb, dyb, xt, dyt, wg, wu, wd, hidden_count, inner,
          interpret=False):
    feature_count, rows, size = xb.shape
    slots = wg.shape[0]
    hshape = (hidden_count, rows, size)
    return pl.pallas_call(
        _front_kernel,
        out_shape=(
            jax.ShapeDtypeStruct((inner, slots // inner, 3, size, size), jnp.bfloat16),
            jax.ShapeDtypeStruct(hshape, jnp.bfloat16),
            jax.ShapeDtypeStruct(hshape, jnp.bfloat16),
            jax.ShapeDtypeStruct(hshape, jnp.bfloat16),
        ),
        in_specs=_specs(3, 7),
        out_specs=tuple(_specs(0, 4)),
        scratch_shapes=[pltpu.VMEM(hshape, jnp.float32)] * 3,
        cost_estimate=pl.CostEstimate(
            flops=6 * slots * 2 * size**3,
            transcendentals=hidden_count * rows * size,
            bytes_accessed=(4 * feature_count * rows + 6 * slots * size + 3 * hidden_count * rows)
            * size * 2,
        ),
        interpret=interpret,
    )(gate_at, up_at, down_at, xb, dyb, xt, dyt, wg, wu, wd)


def back(gate_at, up_at, down_at, hid, gdel, udel, wg, wu, wd, feature_count, interpret=False):
    _, rows, size = hid.shape
    fshape = (feature_count, rows, size)
    return pl.pallas_call(
        _back_kernel,
        out_shape=(
            jax.ShapeDtypeStruct(fshape, jnp.bfloat16),
            jax.ShapeDtypeStruct(fshape, jnp.bfloat16),
        ),
        in_specs=_specs(3, 6),
        out_specs=tuple(_specs(0, 2)),
        scratch_shapes=[pltpu.VMEM(fshape, jnp.float32)] * 2,
        cost_estimate=pl.CostEstimate(
            flops=3 * wg.shape[0] * 2 * size**3,
            transcendentals=0,
            bytes_accessed=(3 * hid.shape[0] * rows + 3 * wg.shape[0] * size + 2 * feature_count * rows)
            * size * 2,
        ),
        interpret=interpret,
    )(gate_at, up_at, down_at, hid, gdel, udel, wg, wu, wd)


def gather_blocks(parts, axis, block_size):
    count = lax.axis_size(axis)
    own = lax.axis_index(axis)
    received = [parts] + [
        lax.ppermute(parts, axis, [(source, (source + shift) % count) for source in range(count)])
        for shift in range(1, count)
    ]
    pieces = jnp.take(jnp.stack(received), (own - jnp.arange(count)) % count, axis=0)
    kinds, rows, width = parts.shape
    pieces = pieces.reshape(count, kinds, rows, width // block_size, block_size)
    blocks = pieces.transpose(1, 0, 3, 2, 4).reshape(kinds, -1, rows, block_size)
    flipped = pieces.transpose(1, 0, 3, 4, 2).reshape(kinds, -1, block_size, rows)
    return blocks, flipped


def scatter_blocks(fulls, axis):
    count = lax.axis_size(axis)
    own = lax.axis_index(axis)
    rows = fulls[0].shape[1]
    pieces = jnp.stack([full.reshape((count, -1) + full.shape[1:]) for full in fulls], 1)
    total = lax.dynamic_index_in_dim(pieces, own, 0, keepdims=False).astype(jnp.float32)
    for shift in range(1, count):
        outgoing = lax.dynamic_index_in_dim(pieces, (own + shift) % count, 0, keepdims=False)
        pairs = [(source, (source + shift) % count) for source in range(count)]
        total = total + lax.ppermute(outgoing, axis, pairs).astype(jnp.float32)
    total = total.astype(jnp.bfloat16)
    return [part.transpose(1, 0, 2).reshape(rows, -1) for part in total]


def reduce_inner(grid, inner):
    count = lax.axis_size(inner)
    own = lax.axis_index(inner)
    total = lax.dynamic_index_in_dim(grid, own, 0, keepdims=False).astype(jnp.float32)
    for shift in range(1, count):
        outgoing = lax.dynamic_index_in_dim(grid, (own + shift) % count, 0, keepdims=False)
        pairs = [(source, (source + shift) % count) for source in range(count)]
        total = total + lax.ppermute(outgoing, inner, pairs).astype(jnp.float32)
    return total.astype(jnp.bfloat16)


def reduce_outer(grid, outer):
    count = lax.axis_size(outer)
    own = lax.axis_index(outer)
    total = lax.dynamic_index_in_dim(grid, own, 0, keepdims=False).astype(jnp.float32)
    for shift in range(1, count):
        outgoing = lax.dynamic_index_in_dim(grid, (own + shift) % count, 0, keepdims=False)
        pairs = [(source, (source + shift) % count) for source in range(count)]
        total = total + lax.ppermute(outgoing, outer, pairs).astype(jnp.float32)
    return total


def layer(
    tokens, grad_out, gate_blocks, gate_values, up_blocks, up_values, down_blocks, down_values
):
    block_size = gate_values.shape[-1]
    tensor_count = lax.axis_size("tensor")
    feature_count = tokens.shape[1] * tensor_count // block_size
    hidden_count = FF // (block_size * tensor_count)
    (inputs, upstream), (inputs_t, upstream_t) = gather_blocks(
        jnp.stack([tokens, grad_out]), "tensor", block_size
    )
    gate_at, up_at, down_at = gate_blocks[0], up_blocks[0], down_blocks[0]
    weights = (gate_values[0], up_values[0], down_values[0])
    stacked, hidden, gate_delta, up_delta = front(
        gate_at, up_at, down_at, inputs, upstream, inputs_t, upstream_t, *weights, hidden_count,
        lax.axis_size("y"),
    )
    partial = reduce_inner(stacked, "y")
    mixed_part, input_part = back(
        gate_at, up_at, down_at, hidden, gate_delta, up_delta, *weights, feature_count
    )
    mixed, grad_tokens = scatter_blocks((mixed_part, input_part), "tensor")
    combined = reduce_outer(partial, "z")[None]
    grad_gate = combined[None, :, 0]
    grad_up = combined[None, :, 1]
    grad_down = combined[None, :, 2].swapaxes(-1, -2)
    return (mixed, grad_tokens, grad_gate, grad_up, grad_down)


def solution(mesh):
    dp_count, tensor_count = mesh.devices.shape
    y_count = len({device.coords[1] for device in mesh.devices[:, 0]})
    split_mesh = Mesh(
        mesh.devices.reshape(dp_count // y_count, y_count, tensor_count), ("z", "y", "tensor")
    )
    dp = ("z", "y")
    in_specs = (
        P(dp, "tensor"),
        P(dp, "tensor"),
        P("tensor", None),
        P("tensor", None, None, None),
        P("tensor", None),
        P("tensor", None, None, None),
        P("tensor", None),
        P("tensor", None, None, None),
    )
    out_specs = (
        P(dp, "tensor"),
        P(dp, "tensor"),
        P("tensor", dp, None, None),
        P("tensor", dp, None, None),
        P("tensor", dp, None, None),
    )
    return jax.shard_map(
        layer, mesh=split_mesh, in_specs=in_specs, out_specs=out_specs, check_vma=False
    )
```

```python
import jax
import jax.numpy as jnp
from jax import lax
from jax.experimental import pallas as pl
from jax.experimental.pallas import tpu as pltpu
from jax.sharding import Mesh
from jax.sharding import PartitionSpec as P

FF = 14336

NT = (((1,), (1,)), ((), ()))


def _dot(a, b, dims=(((1,), (0,)), ((), ()))):
    return lax.dot_general(a, b, dims, preferred_element_type=jnp.float32)


def _front_kernel(gate_at, up_at, down_at, xb, dyb, xt, dyt, wg, wu, wd,
                  terms, hid, gdel, udel, gpre, upre, hgrad):
    inner = terms.shape[0]
    feature_count = xb.shape[0]
    slots = wg.shape[0]
    gpre[...] = jnp.zeros(gpre.shape, jnp.float32)
    upre[...] = jnp.zeros(upre.shape, jnp.float32)
    hgrad[...] = jnp.zeros(hgrad.shape, jnp.float32)

    @pl.loop(0, slots, unroll=8)
    def _(s):
        bg = gate_at[s]

        @pl.when(bg >= 0)
        def _():
            r, c = bg % feature_count, bg // feature_count
            gpre[c] += _dot(xb[r], wg[s])

        bu = up_at[s]

        @pl.when(bu >= 0)
        def _():
            r, c = bu % feature_count, bu // feature_count
            upre[c] += _dot(xb[r], wu[s])

        bd = down_at[s]

        @pl.when(bd >= 0)
        def _():
            r, c = bd % feature_count, bd // feature_count
            hgrad[c] += _dot(dyb[r], wd[s], NT)

    g = gpre[...]
    u = upre[...]
    hg = hgrad[...]
    sig = 1.0 / (1.0 + jnp.exp(-g))
    act = g * sig
    hid[...] = (act * u).astype(hid.dtype)
    gdel[...] = (hg * u * sig * (1.0 + g * (1.0 - sig))).astype(gdel.dtype)
    udel[...] = (hg * act).astype(udel.dtype)

    @pl.loop(0, slots, unroll=8)
    def _(s):
        bg = gate_at[s]

        @pl.when(bg >= 0)
        def _():
            r, c = bg % feature_count, bg // feature_count
            terms[s % inner, s // inner, 0] = _dot(xt[r], gdel[c]).astype(terms.dtype)

        @pl.when(bg < 0)
        def _():
            terms[s % inner, s // inner, 0] = jnp.zeros(terms.shape[3:], terms.dtype)

        bu = up_at[s]

        @pl.when(bu >= 0)
        def _():
            r, c = bu % feature_count, bu // feature_count
            terms[s % inner, s // inner, 1] = _dot(xt[r], udel[c]).astype(terms.dtype)

        @pl.when(bu < 0)
        def _():
            terms[s % inner, s // inner, 1] = jnp.zeros(terms.shape[3:], terms.dtype)

        bd = down_at[s]

        @pl.when(bd >= 0)
        def _():
            r, c = bd % feature_count, bd // feature_count
            terms[s % inner, s // inner, 2] = _dot(dyt[r], hid[c]).astype(terms.dtype)

        @pl.when(bd < 0)
        def _():
            terms[s % inner, s // inner, 2] = jnp.zeros(terms.shape[3:], terms.dtype)


def _back_kernel(gate_at, up_at, down_at, hid, gdel, udel, wg, wu, wd,
                 mixed, grads, macc, iacc):
    feature_count = mixed.shape[0]
    slots = wg.shape[0]
    macc[...] = jnp.zeros(macc.shape, jnp.float32)
    iacc[...] = jnp.zeros(iacc.shape, jnp.float32)

    @pl.loop(0, slots, unroll=8)
    def _(s):
        bd = down_at[s]

        @pl.when(bd >= 0)
        def _():
            r, c = bd % feature_count, bd // feature_count
            macc[r] += _dot(hid[c], wd[s])

        bg = gate_at[s]

        @pl.when(bg >= 0)
        def _():
            r, c = bg % feature_count, bg // feature_count
            iacc[r] += _dot(gdel[c], wg[s], NT)

        bu = up_at[s]

        @pl.when(bu >= 0)
        def _():
            r, c = bu % feature_count, bu // feature_count
            iacc[r] += _dot(udel[c], wu[s], NT)

    mixed[...] = macc[...].astype(mixed.dtype)
    grads[...] = iacc[...].astype(grads.dtype)


def _specs(n_smem, n_vmem):
    return [pl.BlockSpec(memory_space=pltpu.SMEM)] * n_smem + [
        pl.BlockSpec(memory_space=pltpu.VMEM)
    ] * n_vmem


def front(gate_at, up_at, down_at, xb, dyb, xt, dyt, wg, wu, wd, hidden_count, inner,
          interpret=False):
    feature_count, rows, size = xb.shape
    slots = wg.shape[0]
    hshape = (hidden_count, rows, size)
    return pl.pallas_call(
        _front_kernel,
        out_shape=(
            jax.ShapeDtypeStruct((inner, slots // inner, 3, size, size), jnp.bfloat16),
            jax.ShapeDtypeStruct(hshape, jnp.bfloat16),
            jax.ShapeDtypeStruct(hshape, jnp.bfloat16),
            jax.ShapeDtypeStruct(hshape, jnp.bfloat16),
        ),
        in_specs=_specs(3, 7),
        out_specs=tuple(_specs(0, 4)),
        scratch_shapes=[pltpu.VMEM(hshape, jnp.float32)] * 3,
        cost_estimate=pl.CostEstimate(
            flops=6 * slots * 2 * size**3,
            transcendentals=hidden_count * rows * size,
            bytes_accessed=(4 * feature_count * rows + 6 * slots * size + 3 * hidden_count * rows)
            * size * 2,
        ),
        interpret=interpret,
    )(gate_at, up_at, down_at, xb, dyb, xt, dyt, wg, wu, wd)


def back(gate_at, up_at, down_at, hid, gdel, udel, wg, wu, wd, feature_count, interpret=False):
    _, rows, size = hid.shape
    fshape = (feature_count, rows, size)
    return pl.pallas_call(
        _back_kernel,
        out_shape=(
            jax.ShapeDtypeStruct(fshape, jnp.bfloat16),
            jax.ShapeDtypeStruct(fshape, jnp.bfloat16),
        ),
        in_specs=_specs(3, 6),
        out_specs=tuple(_specs(0, 2)),
        scratch_shapes=[pltpu.VMEM(fshape, jnp.float32)] * 2,
        cost_estimate=pl.CostEstimate(
            flops=3 * wg.shape[0] * 2 * size**3,
            transcendentals=0,
            bytes_accessed=(3 * hid.shape[0] * rows + 3 * wg.shape[0] * size + 2 * feature_count * rows)
            * size * 2,
        ),
        interpret=interpret,
    )(gate_at, up_at, down_at, hid, gdel, udel, wg, wu, wd)


def gather_blocks(parts, axis, block_size):
    count = lax.axis_size(axis)
    spread_out = jnp.broadcast_to(parts[None], (count,) + parts.shape)
    pieces = lax.all_to_all(spread_out, axis, 0, 0, tiled=True)
    kinds, rows, width = parts.shape
    pieces = pieces.reshape(count, kinds, rows, width // block_size, block_size)
    blocks = pieces.transpose(1, 0, 3, 2, 4).reshape(kinds, -1, rows, block_size)
    flipped = pieces.transpose(1, 0, 3, 4, 2).reshape(kinds, -1, block_size, rows)
    return blocks, flipped


def scatter_blocks(fulls, axis):
    count = lax.axis_size(axis)
    own = lax.axis_index(axis)
    rows = fulls[0].shape[1]
    pieces = jnp.stack([full.reshape((count, -1) + full.shape[1:]) for full in fulls], 1)
    total = lax.dynamic_index_in_dim(pieces, own, 0, keepdims=False).astype(jnp.float32)
    for shift in range(1, count):
        outgoing = lax.dynamic_index_in_dim(pieces, (own + shift) % count, 0, keepdims=False)
        pairs = [(source, (source + shift) % count) for source in range(count)]
        total = total + lax.ppermute(outgoing, axis, pairs).astype(jnp.float32)
    total = total.astype(jnp.bfloat16)
    return [part.transpose(1, 0, 2).reshape(rows, -1) for part in total]


def reduce_inner(grid, inner):
    count = lax.axis_size(inner)
    own = lax.axis_index(inner)
    total = lax.dynamic_index_in_dim(grid, own, 0, keepdims=False).astype(jnp.float32)
    for shift in range(1, count):
        outgoing = lax.dynamic_index_in_dim(grid, (own + shift) % count, 0, keepdims=False)
        pairs = [(source, (source + shift) % count) for source in range(count)]
        total = total + lax.ppermute(outgoing, inner, pairs).astype(jnp.float32)
    return total.astype(jnp.bfloat16)


def reduce_outer(grid, outer):
    count = lax.axis_size(outer)
    own = lax.axis_index(outer)
    total = lax.dynamic_index_in_dim(grid, own, 0, keepdims=False).astype(jnp.float32)
    for shift in range(1, count):
        outgoing = lax.dynamic_index_in_dim(grid, (own + shift) % count, 0, keepdims=False)
        pairs = [(source, (source + shift) % count) for source in range(count)]
        total = total + lax.ppermute(outgoing, outer, pairs).astype(jnp.float32)
    return total


def layer(
    tokens, grad_out, gate_blocks, gate_values, up_blocks, up_values, down_blocks, down_values
):
    block_size = gate_values.shape[-1]
    tensor_count = lax.axis_size("tensor")
    feature_count = tokens.shape[1] * tensor_count // block_size
    hidden_count = FF // (block_size * tensor_count)
    (inputs, upstream), (inputs_t, upstream_t) = gather_blocks(
        jnp.stack([tokens, grad_out]), "tensor", block_size
    )
    gate_at, up_at, down_at = gate_blocks[0], up_blocks[0], down_blocks[0]
    weights = (gate_values[0], up_values[0], down_values[0])
    stacked, hidden, gate_delta, up_delta = front(
        gate_at, up_at, down_at, inputs, upstream, inputs_t, upstream_t, *weights, hidden_count,
        lax.axis_size("y"),
    )
    partial = reduce_inner(stacked, "y")
    mixed_part, input_part = back(
        gate_at, up_at, down_at, hidden, gate_delta, up_delta, *weights, feature_count
    )
    mixed, grad_tokens = scatter_blocks((mixed_part, input_part), "tensor")
    combined = reduce_outer(partial, "z")[None]
    grad_gate = combined[None, :, 0]
    grad_up = combined[None, :, 1]
    grad_down = combined[None, :, 2].swapaxes(-1, -2)
    return (mixed, grad_tokens, grad_gate, grad_up, grad_down)


def solution(mesh):
    dp_count, tensor_count = mesh.devices.shape
    y_count = len({device.coords[1] for device in mesh.devices[:, 0]})
    split_mesh = Mesh(
        mesh.devices.reshape(dp_count // y_count, y_count, tensor_count), ("z", "y", "tensor")
    )
    dp = ("z", "y")
    in_specs = (
        P(dp, "tensor"),
        P(dp, "tensor"),
        P("tensor", None),
        P("tensor", None, None, None),
        P("tensor", None),
        P("tensor", None, None, None),
        P("tensor", None),
        P("tensor", None, None, None),
    )
    out_specs = (
        P(dp, "tensor"),
        P(dp, "tensor"),
        P("tensor", dp, None, None),
        P("tensor", dp, None, None),
        P("tensor", dp, None, None),
    )
    return jax.shard_map(
        layer, mesh=split_mesh, in_specs=in_specs, out_specs=out_specs, check_vma=False
    )
```

```python
import jax
import jax.numpy as jnp
from jax import lax
from jax.experimental import pallas as pl
from jax.experimental.pallas import tpu as pltpu
from jax.sharding import Mesh
from jax.sharding import PartitionSpec as P

FF = 14336

NT = (((1,), (1,)), ((), ()))


def _dot(a, b, dims=(((1,), (0,)), ((), ()))):
    return lax.dot_general(a, b, dims, preferred_element_type=jnp.float32)


def _front_kernel(gate_at, up_at, down_at, xb, dyb, xt, dyt, wg, wu, wd,
                  terms, hid, gdel, udel, gpre, upre, hgrad):
    inner = terms.shape[0]
    feature_count = xb.shape[0]
    slots = wg.shape[0]
    gpre[...] = jnp.zeros(gpre.shape, jnp.float32)
    upre[...] = jnp.zeros(upre.shape, jnp.float32)
    hgrad[...] = jnp.zeros(hgrad.shape, jnp.float32)

    @pl.loop(0, slots, unroll=4)
    def _(s):
        bg = gate_at[s]

        @pl.when(bg >= 0)
        def _():
            r, c = bg % feature_count, bg // feature_count
            gpre[c] += _dot(xb[r], wg[s])

        bu = up_at[s]

        @pl.when(bu >= 0)
        def _():
            r, c = bu % feature_count, bu // feature_count
            upre[c] += _dot(xb[r], wu[s])

        bd = down_at[s]

        @pl.when(bd >= 0)
        def _():
            r, c = bd % feature_count, bd // feature_count
            hgrad[c] += _dot(dyb[r], wd[s], NT)

    g = gpre[...]
    u = upre[...]
    hg = hgrad[...]
    sig = 1.0 / (1.0 + jnp.exp(-g))
    act = g * sig
    hid[...] = (act * u).astype(hid.dtype)
    gdel[...] = (hg * u * sig * (1.0 + g * (1.0 - sig))).astype(gdel.dtype)
    udel[...] = (hg * act).astype(udel.dtype)

    @pl.loop(0, slots, unroll=4)
    def _(s):
        bg = gate_at[s]

        @pl.when(bg >= 0)
        def _():
            r, c = bg % feature_count, bg // feature_count
            terms[s % inner, s // inner, 0] = _dot(xt[r], gdel[c]).astype(terms.dtype)

        @pl.when(bg < 0)
        def _():
            terms[s % inner, s // inner, 0] = jnp.zeros(terms.shape[3:], terms.dtype)

        bu = up_at[s]

        @pl.when(bu >= 0)
        def _():
            r, c = bu % feature_count, bu // feature_count
            terms[s % inner, s // inner, 1] = _dot(xt[r], udel[c]).astype(terms.dtype)

        @pl.when(bu < 0)
        def _():
            terms[s % inner, s // inner, 1] = jnp.zeros(terms.shape[3:], terms.dtype)

        bd = down_at[s]

        @pl.when(bd >= 0)
        def _():
            r, c = bd % feature_count, bd // feature_count
            terms[s % inner, s // inner, 2] = _dot(dyt[r], hid[c]).astype(terms.dtype)

        @pl.when(bd < 0)
        def _():
            terms[s % inner, s // inner, 2] = jnp.zeros(terms.shape[3:], terms.dtype)


def _back_kernel(gate_at, up_at, down_at, hid, gdel, udel, wg, wu, wd,
                 mixed, grads, macc, iacc):
    feature_count = mixed.shape[0]
    slots = wg.shape[0]
    macc[...] = jnp.zeros(macc.shape, jnp.float32)
    iacc[...] = jnp.zeros(iacc.shape, jnp.float32)

    @pl.loop(0, slots, unroll=4)
    def _(s):
        bd = down_at[s]

        @pl.when(bd >= 0)
        def _():
            r, c = bd % feature_count, bd // feature_count
            macc[r] += _dot(hid[c], wd[s])

        bg = gate_at[s]

        @pl.when(bg >= 0)
        def _():
            r, c = bg % feature_count, bg // feature_count
            iacc[r] += _dot(gdel[c], wg[s], NT)

        bu = up_at[s]

        @pl.when(bu >= 0)
        def _():
            r, c = bu % feature_count, bu // feature_count
            iacc[r] += _dot(udel[c], wu[s], NT)

    mixed[...] = macc[...].astype(mixed.dtype)
    grads[...] = iacc[...].astype(grads.dtype)


def _specs(n_smem, n_vmem):
    return [pl.BlockSpec(memory_space=pltpu.SMEM)] * n_smem + [
        pl.BlockSpec(memory_space=pltpu.VMEM)
    ] * n_vmem


def front(gate_at, up_at, down_at, xb, dyb, xt, dyt, wg, wu, wd, hidden_count, inner,
          interpret=False):
    feature_count, rows, size = xb.shape
    slots = wg.shape[0]
    hshape = (hidden_count, rows, size)
    return pl.pallas_call(
        _front_kernel,
        out_shape=(
            jax.ShapeDtypeStruct((inner, slots // inner, 3, size, size), jnp.bfloat16),
            jax.ShapeDtypeStruct(hshape, jnp.bfloat16),
            jax.ShapeDtypeStruct(hshape, jnp.bfloat16),
            jax.ShapeDtypeStruct(hshape, jnp.bfloat16),
        ),
        in_specs=_specs(3, 7),
        out_specs=tuple(_specs(0, 4)),
        scratch_shapes=[pltpu.VMEM(hshape, jnp.float32)] * 3,
        cost_estimate=pl.CostEstimate(
            flops=6 * slots * 2 * size**3,
            transcendentals=hidden_count * rows * size,
            bytes_accessed=(4 * feature_count * rows + 6 * slots * size + 3 * hidden_count * rows)
            * size * 2,
        ),
        interpret=interpret,
    )(gate_at, up_at, down_at, xb, dyb, xt, dyt, wg, wu, wd)


def back(gate_at, up_at, down_at, hid, gdel, udel, wg, wu, wd, feature_count, interpret=False):
    _, rows, size = hid.shape
    fshape = (feature_count, rows, size)
    return pl.pallas_call(
        _back_kernel,
        out_shape=(
            jax.ShapeDtypeStruct(fshape, jnp.bfloat16),
            jax.ShapeDtypeStruct(fshape, jnp.bfloat16),
        ),
        in_specs=_specs(3, 6),
        out_specs=tuple(_specs(0, 2)),
        scratch_shapes=[pltpu.VMEM(fshape, jnp.float32)] * 2,
        cost_estimate=pl.CostEstimate(
            flops=3 * wg.shape[0] * 2 * size**3,
            transcendentals=0,
            bytes_accessed=(3 * hid.shape[0] * rows + 3 * wg.shape[0] * size + 2 * feature_count * rows)
            * size * 2,
        ),
        interpret=interpret,
    )(gate_at, up_at, down_at, hid, gdel, udel, wg, wu, wd)


def gather_blocks(parts, axis, block_size):
    count = lax.axis_size(axis)
    kinds, rows, width = parts.shape
    local = parts.reshape(kinds, rows, width // block_size, block_size).transpose(0, 2, 1, 3)
    spread_out = jnp.broadcast_to(local[None], (count,) + local.shape)
    pieces = lax.all_to_all(spread_out, axis, 0, 0, tiled=True)
    blocks = pieces.transpose(1, 0, 2, 3, 4).reshape(kinds, -1, rows, block_size)
    return blocks, blocks.swapaxes(-1, -2)


def scatter_blocks(fulls, axis):
    count = lax.axis_size(axis)
    own = lax.axis_index(axis)
    rows = fulls[0].shape[1]
    pieces = jnp.stack([full.reshape((count, -1) + full.shape[1:]) for full in fulls], 1)
    total = lax.dynamic_index_in_dim(pieces, own, 0, keepdims=False).astype(jnp.float32)
    for shift in range(1, count):
        outgoing = lax.dynamic_index_in_dim(pieces, (own + shift) % count, 0, keepdims=False)
        pairs = [(source, (source + shift) % count) for source in range(count)]
        total = total + lax.ppermute(outgoing, axis, pairs).astype(jnp.float32)
    total = total.astype(jnp.bfloat16)
    return [part.transpose(1, 0, 2).reshape(rows, -1) for part in total]


def reduce_inner(grid, inner):
    count = lax.axis_size(inner)
    own = lax.axis_index(inner)
    total = lax.dynamic_index_in_dim(grid, own, 0, keepdims=False).astype(jnp.float32)
    for shift in range(1, count):
        outgoing = lax.dynamic_index_in_dim(grid, (own + shift) % count, 0, keepdims=False)
        pairs = [(source, (source + shift) % count) for source in range(count)]
        total = total + lax.ppermute(outgoing, inner, pairs).astype(jnp.float32)
    return total.astype(jnp.bfloat16)


def reduce_outer(grid, outer):
    count = lax.axis_size(outer)
    own = lax.axis_index(outer)
    total = lax.dynamic_index_in_dim(grid, own, 0, keepdims=False).astype(jnp.float32)
    for shift in range(1, count):
        outgoing = lax.dynamic_index_in_dim(grid, (own + shift) % count, 0, keepdims=False)
        pairs = [(source, (source + shift) % count) for source in range(count)]
        total = total + lax.ppermute(outgoing, outer, pairs).astype(jnp.float32)
    return total


def layer(
    tokens, grad_out, gate_blocks, gate_values, up_blocks, up_values, down_blocks, down_values
):
    block_size = gate_values.shape[-1]
    tensor_count = lax.axis_size("tensor")
    feature_count = tokens.shape[1] * tensor_count // block_size
    hidden_count = FF // (block_size * tensor_count)
    (inputs, upstream), (inputs_t, upstream_t) = gather_blocks(
        jnp.stack([tokens, grad_out]), "tensor", block_size
    )
    gate_at, up_at, down_at = gate_blocks[0], up_blocks[0], down_blocks[0]
    weights = (gate_values[0], up_values[0], down_values[0])
    stacked, hidden, gate_delta, up_delta = front(
        gate_at, up_at, down_at, inputs, upstream, inputs_t, upstream_t, *weights, hidden_count,
        lax.axis_size("y"),
    )
    partial = reduce_inner(stacked, "y")
    mixed_part, input_part = back(
        gate_at, up_at, down_at, hidden, gate_delta, up_delta, *weights, feature_count
    )
    mixed, grad_tokens = scatter_blocks((mixed_part, input_part), "tensor")
    combined = reduce_outer(partial, "z")[None]
    grad_gate = combined[None, :, 0]
    grad_up = combined[None, :, 1]
    grad_down = combined[None, :, 2].swapaxes(-1, -2)
    return (mixed, grad_tokens, grad_gate, grad_up, grad_down)


def solution(mesh):
    dp_count, tensor_count = mesh.devices.shape
    y_count = len({device.coords[1] for device in mesh.devices[:, 0]})
    split_mesh = Mesh(
        mesh.devices.reshape(dp_count // y_count, y_count, tensor_count), ("z", "y", "tensor")
    )
    dp = ("z", "y")
    in_specs = (
        P(dp, "tensor"),
        P(dp, "tensor"),
        P("tensor", None),
        P("tensor", None, None, None),
        P("tensor", None),
        P("tensor", None, None, None),
        P("tensor", None),
        P("tensor", None, None, None),
    )
    out_specs = (
        P(dp, "tensor"),
        P(dp, "tensor"),
        P("tensor", dp, None, None),
        P("tensor", dp, None, None),
        P("tensor", dp, None, None),
    )
    return jax.shard_map(
        layer, mesh=split_mesh, in_specs=in_specs, out_specs=out_specs, check_vma=False
    )
```

```python
import jax
import jax.numpy as jnp
from jax import lax
from jax.experimental import pallas as pl
from jax.experimental.pallas import tpu as pltpu
from jax.sharding import Mesh
from jax.sharding import PartitionSpec as P

FF = 14336

NT = (((1,), (1,)), ((), ()))


def _dot(a, b, dims=(((1,), (0,)), ((), ()))):
    return lax.dot_general(a, b, dims, preferred_element_type=jnp.float32)


def _front_kernel(gate_at, up_at, down_at, xb, dyb, xt, dyt, wg, wu, wd,
                  terms, hid, gdel, udel, gpre, upre, hgrad):
    inner = terms.shape[0]
    feature_count = xb.shape[0]
    slots = wg.shape[0]
    gpre[...] = jnp.zeros(gpre.shape, jnp.float32)
    upre[...] = jnp.zeros(upre.shape, jnp.float32)
    hgrad[...] = jnp.zeros(hgrad.shape, jnp.float32)

    @pl.loop(0, slots, unroll=4)
    def _(s):
        bg = gate_at[s]

        @pl.when(bg >= 0)
        def _():
            r, c = bg % feature_count, bg // feature_count
            gpre[c] += _dot(xb[r], wg[s])

        bu = up_at[s]

        @pl.when(bu >= 0)
        def _():
            r, c = bu % feature_count, bu // feature_count
            upre[c] += _dot(xb[r], wu[s])

        bd = down_at[s]

        @pl.when(bd >= 0)
        def _():
            r, c = bd % feature_count, bd // feature_count
            hgrad[c] += _dot(dyb[r], wd[s], NT)

    g = gpre[...]
    u = upre[...]
    hg = hgrad[...]
    sig = 1.0 / (1.0 + jnp.exp(-g))
    act = g * sig
    hid[...] = (act * u).astype(hid.dtype)
    gdel[...] = (hg * u * sig * (1.0 + g * (1.0 - sig))).astype(gdel.dtype)
    udel[...] = (hg * act).astype(udel.dtype)

    @pl.loop(0, slots, unroll=4)
    def _(s):
        bg = gate_at[s]

        @pl.when(bg >= 0)
        def _():
            r, c = bg % feature_count, bg // feature_count
            terms[s % inner, s // inner, 0] = _dot(xt[r], gdel[c]).astype(terms.dtype)

        @pl.when(bg < 0)
        def _():
            terms[s % inner, s // inner, 0] = jnp.zeros(terms.shape[3:], terms.dtype)

        bu = up_at[s]

        @pl.when(bu >= 0)
        def _():
            r, c = bu % feature_count, bu // feature_count
            terms[s % inner, s // inner, 1] = _dot(xt[r], udel[c]).astype(terms.dtype)

        @pl.when(bu < 0)
        def _():
            terms[s % inner, s // inner, 1] = jnp.zeros(terms.shape[3:], terms.dtype)

        bd = down_at[s]

        @pl.when(bd >= 0)
        def _():
            r, c = bd % feature_count, bd // feature_count
            terms[s % inner, s // inner, 2] = _dot(dyt[r], hid[c]).astype(terms.dtype)

        @pl.when(bd < 0)
        def _():
            terms[s % inner, s // inner, 2] = jnp.zeros(terms.shape[3:], terms.dtype)


def _back_kernel(gate_at, up_at, down_at, hid, gdel, udel, wg, wu, wd,
                 mixed, grads, macc, iacc):
    feature_count = mixed.shape[0]
    slots = wg.shape[0]
    macc[...] = jnp.zeros(macc.shape, jnp.float32)
    iacc[...] = jnp.zeros(iacc.shape, jnp.float32)

    @pl.loop(0, slots, unroll=4)
    def _(s):
        bd = down_at[s]

        @pl.when(bd >= 0)
        def _():
            r, c = bd % feature_count, bd // feature_count
            macc[r] += _dot(hid[c], wd[s])

        bg = gate_at[s]

        @pl.when(bg >= 0)
        def _():
            r, c = bg % feature_count, bg // feature_count
            iacc[r] += _dot(gdel[c], wg[s], NT)

        bu = up_at[s]

        @pl.when(bu >= 0)
        def _():
            r, c = bu % feature_count, bu // feature_count
            iacc[r] += _dot(udel[c], wu[s], NT)

    mixed[...] = macc[...].astype(mixed.dtype)
    grads[...] = iacc[...].astype(grads.dtype)


def _specs(n_smem, n_vmem):
    return [pl.BlockSpec(memory_space=pltpu.SMEM)] * n_smem + [
        pl.BlockSpec(memory_space=pltpu.VMEM)
    ] * n_vmem


def front(gate_at, up_at, down_at, xb, dyb, xt, dyt, wg, wu, wd, hidden_count, inner,
          interpret=False):
    feature_count, rows, size = xb.shape
    slots = wg.shape[0]
    hshape = (hidden_count, rows, size)
    return pl.pallas_call(
        _front_kernel,
        out_shape=(
            jax.ShapeDtypeStruct((inner, slots // inner, 3, size, size), jnp.bfloat16),
            jax.ShapeDtypeStruct(hshape, jnp.bfloat16),
            jax.ShapeDtypeStruct(hshape, jnp.bfloat16),
            jax.ShapeDtypeStruct(hshape, jnp.bfloat16),
        ),
        in_specs=_specs(3, 7),
        out_specs=tuple(_specs(0, 4)),
        scratch_shapes=[pltpu.VMEM(hshape, jnp.float32)] * 3,
        cost_estimate=pl.CostEstimate(
            flops=6 * slots * 2 * size**3,
            transcendentals=hidden_count * rows * size,
            bytes_accessed=(4 * feature_count * rows + 6 * slots * size + 3 * hidden_count * rows)
            * size * 2,
        ),
        interpret=interpret,
    )(gate_at, up_at, down_at, xb, dyb, xt, dyt, wg, wu, wd)


def back(gate_at, up_at, down_at, hid, gdel, udel, wg, wu, wd, feature_count, interpret=False):
    _, rows, size = hid.shape
    fshape = (feature_count, rows, size)
    return pl.pallas_call(
        _back_kernel,
        out_shape=(
            jax.ShapeDtypeStruct(fshape, jnp.bfloat16),
            jax.ShapeDtypeStruct(fshape, jnp.bfloat16),
        ),
        in_specs=_specs(3, 6),
        out_specs=tuple(_specs(0, 2)),
        scratch_shapes=[pltpu.VMEM(fshape, jnp.float32)] * 2,
        cost_estimate=pl.CostEstimate(
            flops=3 * wg.shape[0] * 2 * size**3,
            transcendentals=0,
            bytes_accessed=(3 * hid.shape[0] * rows + 3 * wg.shape[0] * size + 2 * feature_count * rows)
            * size * 2,
        ),
        interpret=interpret,
    )(gate_at, up_at, down_at, hid, gdel, udel, wg, wu, wd)


def gather_blocks(parts, axis, block_size):
    count = lax.axis_size(axis)
    spread_out = jnp.broadcast_to(parts[None], (count,) + parts.shape)
    pieces = lax.all_to_all(spread_out, axis, 0, 0, tiled=True)
    kinds, rows, width = parts.shape
    pieces = pieces.reshape(count, kinds, rows, width // block_size, block_size)
    blocks = pieces.transpose(1, 0, 3, 2, 4).reshape(kinds, -1, rows, block_size)
    flipped = pieces.transpose(1, 0, 3, 4, 2).reshape(kinds, -1, block_size, rows)
    return blocks, flipped


def scatter_blocks(fulls, axis):
    count = lax.axis_size(axis)
    own = lax.axis_index(axis)
    rows = fulls[0].shape[1]
    pieces = jnp.stack([full.reshape((count, -1) + full.shape[1:]) for full in fulls], 1)
    total = lax.dynamic_index_in_dim(pieces, own, 0, keepdims=False).astype(jnp.float32)
    for shift in range(1, count):
        outgoing = lax.dynamic_index_in_dim(pieces, (own + shift) % count, 0, keepdims=False)
        pairs = [(source, (source + shift) % count) for source in range(count)]
        total = total + lax.ppermute(outgoing, axis, pairs).astype(jnp.float32)
    total = total.astype(jnp.bfloat16)
    return [part.transpose(1, 0, 2).reshape(rows, -1) for part in total]


def reduce_inner(grid, inner):
    count = lax.axis_size(inner)
    own = lax.axis_index(inner)
    total = lax.dynamic_index_in_dim(grid, own, 0, keepdims=False).astype(jnp.float32)
    for shift in range(1, count):
        outgoing = lax.dynamic_index_in_dim(grid, (own + shift) % count, 0, keepdims=False)
        pairs = [(source, (source + shift) % count) for source in range(count)]
        total = total + lax.ppermute(outgoing, inner, pairs).astype(jnp.float32)
    return total.astype(jnp.bfloat16)


def reduce_outer(grid, outer):
    count = lax.axis_size(outer)
    own = lax.axis_index(outer)
    total = lax.dynamic_index_in_dim(grid, own, 0, keepdims=False).astype(jnp.float32)
    for shift in range(1, count):
        outgoing = lax.dynamic_index_in_dim(grid, (own + shift) % count, 0, keepdims=False)
        pairs = [(source, (source + shift) % count) for source in range(count)]
        total = total + lax.ppermute(outgoing, outer, pairs).astype(jnp.float32)
    return total


def layer(
    tokens, grad_out, gate_blocks, gate_values, up_blocks, up_values, down_blocks, down_values
):
    block_size = gate_values.shape[-1]
    tensor_count = lax.axis_size("tensor")
    feature_count = tokens.shape[1] * tensor_count // block_size
    hidden_count = FF // (block_size * tensor_count)
    (inputs, upstream), (inputs_t, upstream_t) = gather_blocks(
        jnp.stack([tokens, grad_out]), "tensor", block_size
    )
    gate_at, up_at, down_at = gate_blocks[0], up_blocks[0], down_blocks[0]
    weights = (gate_values[0], up_values[0], down_values[0])
    stacked, hidden, gate_delta, up_delta = front(
        gate_at, up_at, down_at, inputs, upstream, inputs_t, upstream_t, *weights, hidden_count,
        lax.axis_size("y"),
    )
    partial = reduce_inner(stacked, "y")
    mixed_part, input_part = back(
        gate_at, up_at, down_at, hidden, gate_delta, up_delta, *weights, feature_count
    )
    mixed, grad_tokens = scatter_blocks((mixed_part, input_part), "tensor")
    combined = reduce_outer(partial, "z")[None]
    grad_gate = combined[None, :, 0]
    grad_up = combined[None, :, 1]
    grad_down = combined[None, :, 2].swapaxes(-1, -2)
    return (mixed, grad_tokens, grad_gate, grad_up, grad_down)


def solution(mesh):
    dp_count, tensor_count = mesh.devices.shape
    y_count = len({device.coords[1] for device in mesh.devices[:, 0]})
    split_mesh = Mesh(
        mesh.devices.reshape(dp_count // y_count, y_count, tensor_count), ("z", "y", "tensor")
    )
    dp = ("z", "y")
    in_specs = (
        P(dp, "tensor"),
        P(dp, "tensor"),
        P("tensor", None),
        P("tensor", None, None, None),
        P("tensor", None),
        P("tensor", None, None, None),
        P("tensor", None),
        P("tensor", None, None, None),
    )
    out_specs = (
        P(dp, "tensor"),
        P(dp, "tensor"),
        P("tensor", dp, None, None),
        P("tensor", dp, None, None),
        P("tensor", dp, None, None),
    )
    return jax.shard_map(
        layer, mesh=split_mesh, in_specs=in_specs, out_specs=out_specs, check_vma=False
    )
```
